32 devices in a mesh: dp: 8 (over z, y), tensor: 4 (over x, core).
Axes of the slice: x: 2, y: 2, z: 4, core: 2. Of those that a mesh axis runs over, the one named last changes fastest.
Arguments:
- inputs: bfloat16 [1024, 8192], P('dp', 'tensor'), may hold values from -6 to 6
- cotangent: bfloat16 [1024, 1024], P('dp', 'tensor'), may hold values from -6 to 6
- frozen_key_weight: bfloat16 [8192, 1024], P(None, 'tensor'), may hold values from -0.1875 to 0.1875
- adapter_down_weight: bfloat16 [8, 16, 8192], P('dp', None, 'tensor'), may hold values from -0.0625 to 0.0625
- adapter_up_weight: bfloat16 [8, 16, 1024], P('dp', None, 'tensor'), may hold values from -0.1875 to 0.1875
- tenant_per_block: int32 [8], P('dp'), may hold values from 0 to 7
Outputs:
- grad_inputs: bfloat16 [1024, 8192], P('dp', 'tensor')
- grad_down: float32 [8, 16, 8192], P('dp', None, 'tensor')
- grad_up: float32 [8, 16, 1024], P('dp', None, 'tensor')
The draws below stay inside these ranges and needn't reach their ends.
All inputs are finite; a program needn't handle non-finite values.
Results may differ from the reference program's by a relative error of at most 0.0034.
Values may be sent and summed in bfloat16 or wider, within the bound.
No kernel may reach another device: no remote copies, remote signals or barrier semaphores. Data moves between devices by JAX's collectives and lax.ppermute only.
A program may use at most 128 MiB of HBM per device.

```python
import math
import jax
import jax.numpy as jnp
import numpy as np
from jax import lax

MODEL_WIDTH = 8192
KEY_WIDTH = 1024
ADAPTER_RANK = 16
BLOCK_ROWS = 128
TENANT_TOTAL = 8
TOKENS = 1024
BLOCKS = 8


def touch_ends(entries, stream_key, least, top_value):
    shape = entries.shape
    place = [jax.random.randint(jax.random.fold_in(stream_key, axis), (), 0, shape[axis]) for axis in range(len(shape))]
    entries = entries.at[tuple(place)].set(least)
    longest = shape.index(max(shape))
    place[longest] = (place[longest] + 1) % shape[longest]
    return entries.at[tuple(place)].set(top_value)


def shard_levels(rng, shape, split, low, high):
    level, own = 1.0, jax.random.fold_in(rng, 6)
    for dim, shards_of in split:
        heights = jnp.exp(jax.random.uniform(jax.random.fold_in(own, dim), (shards_of,), jnp.float32, low / len(split), high / len(split)))
        level = level * jnp.repeat(heights, shape[dim] // shards_of).reshape([-1 if axis == dim else 1 for axis in range(len(shape))])
    return level


def cumulative_ranks(number_of, skew):
    portions = [(1 << 20) // math.isqrt(rank ** skew) + 1 for rank in range(1, number_of + 1)]
    scale = 1 + sum(portions) // (1 << 30)
    return np.cumsum(np.array([max(1, weight // scale) for weight in portions]))


def skewed_ids(key, extent, amount, lean):
    grid = cumulative_ranks(amount, lean)
    ticket = jax.random.randint(jax.random.fold_in(key, 1), extent, 0, int(grid[amount - 1]))
    standing = jnp.searchsorted(jnp.asarray(grid, jnp.int32), ticket, side="right")
    return jax.random.permutation(jax.random.fold_in(key, 2), amount)[standing].astype(jnp.int32)


def noise(stream_key, shape, scale, limit, split=(), held_as=jnp.bfloat16):
    array = jax.random.normal(stream_key, shape, jnp.float32) * scale
    if len(split) > 0:
        array = shard_levels(stream_key, shape, split, -0.22, 0.18) * array
    return jnp.clip(array, min=-limit, max=limit).astype(held_as)


def setup_inputs(seed: int = 0) -> dict:
    splits = jax.random.split(jax.random.key(seed), 7)
    inputs = noise(splits[0], (TOKENS, MODEL_WIDTH), 1.0, 6.0, ((0, 8), (1, 4)))
    cotangent = noise(splits[1], (TOKENS, KEY_WIDTH), 1.0, 6.0, ((0, 8), (1, 4)))
    frozen_key_weight = noise(splits[2], (MODEL_WIDTH, KEY_WIDTH), KEY_WIDTH ** -0.5, 0.1875, ((1, 4),))
    adapter_down_weight = noise(splits[3], (TENANT_TOTAL, ADAPTER_RANK, MODEL_WIDTH), MODEL_WIDTH ** -0.5, 0.0625, ((0, 8), (2, 4)))
    adapter_up_weight = noise(splits[4], (TENANT_TOTAL, ADAPTER_RANK, KEY_WIDTH), KEY_WIDTH ** -0.5, 0.1875, ((0, 8), (2, 4)))
    tenant_per_block = touch_ends(skewed_ids(splits[5], (BLOCKS,), TENANT_TOTAL, 2), jax.random.fold_in(splits[5], 3), 0, TENANT_TOTAL - 1).astype(jnp.int32)
    return dict(inputs=inputs, cotangent=cotangent, frozen_key_weight=frozen_key_weight, adapter_down_weight=adapter_down_weight, adapter_up_weight=adapter_up_weight, tenant_per_block=tenant_per_block)


ADAPTER_SCALE = 2.0


def reference(inputs, cotangent, frozen_key_weight, adapter_down_weight, adapter_up_weight, tenant_per_block):
    input_blocks = inputs.reshape(BLOCKS, BLOCK_ROWS, MODEL_WIDTH)
    cotangent_blocks = cotangent.reshape(BLOCKS, BLOCK_ROWS, KEY_WIDTH)

    def per_block(item):
        x_rows, gradient_rows, current_tenant = item
        down_matrix = lax.dynamic_index_in_dim(adapter_down_weight, current_tenant.astype(jnp.int32), 0, keepdims=False)
        up_matrix = lax.dynamic_index_in_dim(adapter_up_weight, current_tenant.astype(jnp.int32), 0, keepdims=False)
        low_in = jnp.dot(x_rows, down_matrix.T, preferred_element_type=jnp.float32)
        reduced_output = ADAPTER_SCALE * jnp.dot(gradient_rows, up_matrix.T, preferred_element_type=jnp.float32)
        reduced_input_batch = low_in.astype(jnp.bfloat16)
        low_out_b = reduced_output.astype(jnp.bfloat16)
        grad_rows = jnp.dot(gradient_rows, frozen_key_weight.T, preferred_element_type=jnp.float32)
        grad_rows = grad_rows + jnp.dot(low_out_b, down_matrix, preferred_element_type=jnp.float32)
        down_term = jnp.dot(low_out_b.T, x_rows, preferred_element_type=jnp.float32)
        up_partial_product = ADAPTER_SCALE * jnp.dot(reduced_input_batch.T, gradient_rows, preferred_element_type=jnp.float32)
        return grad_rows.astype(jnp.bfloat16), down_term, up_partial_product

    grad_blocks, down_terms, up_terms = lax.map(per_block, (input_blocks, cotangent_blocks, tenant_per_block))
    grad_inputs = grad_blocks.reshape(TOKENS, MODEL_WIDTH)
    grad_down = jax.ops.segment_sum(down_terms, tenant_per_block, num_segments=TENANT_TOTAL)
    grad_up = jax.ops.segment_sum(up_terms, tenant_per_block, num_segments=TENANT_TOTAL)
    return grad_inputs, grad_down, grad_up
```

```python
import jax
import jax.numpy as jnp
from jax import lax
from jax.sharding import PartitionSpec as P

ADAPTER_SCALE = 2.0


def _partners(size):
    if size & (size - 1) == 0:
        return [(s, [(i, i ^ s) for i in range(size)]) for s in range(1, size)]
    return [(s, [(i, (i + s) % size) for i in range(size)]) for s in range(1, size)]


def _source_of(me, shift, size):
    if size & (size - 1) == 0:
        return me ^ shift
    return (me - shift + size) % size


def _dest_of(me, shift, size):
    if size & (size - 1) == 0:
        return me ^ shift
    return (me + shift) % size


def _gather_dp(local, axis, size):
    me = lax.axis_index(axis)
    got = [local]
    sources = [me]
    for shift, pairs in _partners(size):
        got.append(lax.ppermute(local, axis, pairs))
        sources.append(_source_of(me, shift, size))
    stacked = jnp.stack(got, 0)
    order = jnp.stack(sources)
    return stacked, order


def _psum_small(value, axis, size):
    total = value
    for _, pairs in _partners(size):
        total = total + lax.ppermute(value, axis, pairs)
    return total


def _reduce_scatter_cols(partial, axis, size):
    rows, cols = partial.shape
    if size & (size - 1) != 0:
        return lax.psum_scatter(partial, axis, scatter_dimension=1, tiled=True)
    me = lax.axis_index(axis)
    held = partial.reshape(rows, size, cols // size)
    bit = 0
    while (1 << bit) < size:
        width = held.shape[1] // 2
        split = held.reshape(rows, width, 2, cols // size)
        mine = (me >> bit) & 1
        keep = lax.dynamic_index_in_dim(split, mine, 2, keepdims=False)
        give = lax.dynamic_index_in_dim(split, 1 - mine, 2, keepdims=False)
        partner = 1 << bit
        got = lax.ppermute(give, axis, [(i, i ^ partner) for i in range(size)])
        held = keep + got
        bit += 1
    return held.reshape(rows, cols // size)


def on_device(
    inputs, cotangent, frozen_key_weight, adapter_down_weight, adapter_up_weight, tenant_per_block
):
    token_row_count, width_portion = inputs.shape
    key_portion = cotangent.shape[1]
    block_count = tenant_per_block.shape[0]
    block_rows = token_row_count // block_count
    adapter_rank_size = adapter_down_weight.shape[1]
    held_tenants = adapter_down_weight.shape[0]
    dp_size = lax.axis_size("dp")
    tensor_size = lax.axis_size("tensor")
    tenant_number = dp_size * held_tenants
    me_dp = lax.axis_index("dp")

    partial_grad = lax.dot_general(
        cotangent, frozen_key_weight, (((1,), (1,)), ((), ())), preferred_element_type=jnp.float32
    )
    base_grad = _reduce_scatter_cols(partial_grad, "tensor", tensor_size)

    packed = jnp.concatenate([adapter_down_weight, adapter_up_weight], axis=2)
    stacked, order = _gather_dp(packed, "dp", dp_size)
    owner = tenant_per_block // held_tenants
    local = tenant_per_block % held_tenants
    pick = (order[None, :] == owner[:, None])
    pick = pick[:, :, None] & (jnp.arange(held_tenants)[None, None, :] == local[:, None, None])
    pick = pick.reshape(block_count, dp_size * held_tenants).astype(jnp.bfloat16)
    flat = stacked.reshape(dp_size * held_tenants, adapter_rank_size, width_portion + key_portion)
    selected = jnp.einsum("bk,krd->brd", pick, flat, preferred_element_type=jnp.float32).astype(jnp.bfloat16)
    sel_down = selected[:, :, :width_portion]
    sel_up = selected[:, :, width_portion:]

    input_blocks = inputs.reshape(block_count, block_rows, width_portion)
    cotangent_blocks = cotangent.reshape(block_count, block_rows, key_portion)
    low_in = jnp.einsum("bnd,brd->bnr", input_blocks, sel_down, preferred_element_type=jnp.float32)
    reduced_output = ADAPTER_SCALE * jnp.einsum(
        "bnk,brk->bnr", cotangent_blocks, sel_up, preferred_element_type=jnp.float32
    )
    lows = _psum_small(jnp.concatenate([low_in, reduced_output], axis=2), "tensor", tensor_size)
    reduced_input_batch = lows[:, :, :adapter_rank_size].astype(jnp.bfloat16)
    low_out_b = lows[:, :, adapter_rank_size:].astype(jnp.bfloat16)

    adapter_grad = jnp.einsum(
        "bnr,brd->bnd", low_out_b, sel_down, preferred_element_type=jnp.float32
    )
    adapter_grad = adapter_grad.reshape(token_row_count, width_portion)
    grad_inputs = (base_grad + adapter_grad).astype(jnp.bfloat16)

    all_tenants = jnp.arange(tenant_number, dtype=jnp.int32)
    member = tenant_per_block[:, None] == all_tenants[None, :]
    member_b = member.astype(jnp.bfloat16)
    weighted_out = (member_b[:, None, :, None] * low_out_b[:, :, None, :]).reshape(
        token_row_count, tenant_number * adapter_rank_size
    )
    weighted_in = (member_b[:, None, :, None] * reduced_input_batch[:, :, None, :]).reshape(
        token_row_count, tenant_number * adapter_rank_size
    )
    down_contribution = lax.dot_general(
        weighted_out, inputs, (((0,), (0,)), ((), ())), preferred_element_type=jnp.float32
    )
    up_contribution = ADAPTER_SCALE * lax.dot_general(
        weighted_in, cotangent, (((0,), (0,)), ((), ())), preferred_element_type=jnp.float32
    )
    down_contribution = down_contribution.reshape(dp_size, held_tenants, adapter_rank_size, width_portion)
    up_contribution = up_contribution.reshape(dp_size, held_tenants, adapter_rank_size, key_portion)
    combined = jnp.concatenate([down_contribution, up_contribution], axis=3)
    owned = lax.dynamic_index_in_dim(combined, me_dp, 0, keepdims=False)
    for shift, pairs in _partners(dp_size):
        outgoing = lax.dynamic_index_in_dim(combined, _dest_of(me_dp, shift, dp_size), 0, keepdims=False)
        owned = owned + lax.ppermute(outgoing, "dp", pairs)
    grad_down = owned[:, :, :width_portion]
    grad_up = owned[:, :, width_portion:]
    return (grad_inputs, grad_down, grad_up)


def solution(mesh):
    in_specs = (
        P("dp", "tensor"),
        P("dp", "tensor"),
        P(None, "tensor"),
        P("dp", None, "tensor"),
        P("dp", None, "tensor"),
        P("dp"),
    )
    out_specs = (P("dp", "tensor"), P("dp", None, "tensor"), P("dp", None, "tensor"))
    return jax.shard_map(
        on_device, mesh=mesh, in_specs=in_specs, out_specs=out_specs, check_vma=False
    )
```

```python
import jax
import jax.numpy as jnp
from jax import lax
from jax.sharding import PartitionSpec as P

ADAPTER_SCALE = 2.0


def _partners(size):
    if size & (size - 1) == 0:
        return [(s, [(i, i ^ s) for i in range(size)]) for s in range(1, size)]
    return [(s, [(i, (i + s) % size) for i in range(size)]) for s in range(1, size)]


def _source_of(me, shift, size):
    if size & (size - 1) == 0:
        return me ^ shift
    return (me - shift + size) % size


def _dest_of(me, shift, size):
    if size & (size - 1) == 0:
        return me ^ shift
    return (me + shift) % size


def _gather_dp(local, axis, size):
    me = lax.axis_index(axis)
    got = [local]
    sources = [me]
    for shift, pairs in _partners(size):
        got.append(lax.ppermute(local, axis, pairs))
        sources.append(_source_of(me, shift, size))
    stacked = jnp.stack(got, 0)
    order = jnp.stack(sources)
    return stacked, order


def _psum_small(value, axis, size):
    total = value
    for _, pairs in _partners(size):
        total = total + lax.ppermute(value, axis, pairs)
    return total


def _frozen_term(cotangent, weight, axis, size):
    if size & (size - 1) != 0:
        partial = lax.dot_general(
            cotangent, weight, (((1,), (1,)), ((), ())), preferred_element_type=jnp.float32
        )
        return lax.psum_scatter(partial, axis, scatter_dimension=1, tiled=True)
    me = lax.axis_index(axis)
    rows = weight.shape[0] // size

    def term(block):
        piece = lax.dynamic_slice_in_dim(weight, block * rows, rows, axis=0)
        return lax.dot_general(
            cotangent, piece, (((1,), (1,)), ((), ())), preferred_element_type=jnp.float32
        )

    held = [term(me ^ e) for e in range(size)]
    step = 0
    while len(held) > 1:
        partner = 1 << step
        pairs = [(i, i ^ partner) for i in range(size)]
        got = [lax.ppermute(held[e], axis, pairs) for e in range(1, len(held), 2)]
        held = [held[e] + g for e, g in zip(range(0, len(held), 2), got)]
        step += 1
    return held[0]


def on_device(
    inputs, cotangent, frozen_key_weight, adapter_down_weight, adapter_up_weight, tenant_per_block
):
    token_row_count, width_portion = inputs.shape
    key_portion = cotangent.shape[1]
    block_count = tenant_per_block.shape[0]
    block_rows = token_row_count // block_count
    adapter_rank_size = adapter_down_weight.shape[1]
    held_tenants = adapter_down_weight.shape[0]
    dp_size = lax.axis_size("dp")
    tensor_size = lax.axis_size("tensor")
    tenant_number = dp_size * held_tenants
    me_dp = lax.axis_index("dp")

    base_grad = _frozen_term(cotangent, frozen_key_weight, "tensor", tensor_size)

    packed = jnp.concatenate([adapter_down_weight, adapter_up_weight], axis=2)
    stacked, order = _gather_dp(packed, "dp", dp_size)
    owner = tenant_per_block // held_tenants
    local = tenant_per_block % held_tenants
    pick = (order[None, :] == owner[:, None])
    pick = pick[:, :, None] & (jnp.arange(held_tenants)[None, None, :] == local[:, None, None])
    pick = pick.reshape(block_count, dp_size * held_tenants).astype(jnp.bfloat16)
    flat = stacked.reshape(dp_size * held_tenants, adapter_rank_size, width_portion + key_portion)
    selected = jnp.einsum("bk,krd->brd", pick, flat, preferred_element_type=jnp.float32).astype(jnp.bfloat16)
    sel_down = selected[:, :, :width_portion]
    sel_up = selected[:, :, width_portion:]

    input_blocks = inputs.reshape(block_count, block_rows, width_portion)
    cotangent_blocks = cotangent.reshape(block_count, block_rows, key_portion)
    low_in = jnp.einsum("bnd,brd->bnr", input_blocks, sel_down, preferred_element_type=jnp.float32)
    reduced_output = ADAPTER_SCALE * jnp.einsum(
        "bnk,brk->bnr", cotangent_blocks, sel_up, preferred_element_type=jnp.float32
    )
    lows = _psum_small(jnp.concatenate([low_in, reduced_output], axis=2), "tensor", tensor_size)
    reduced_input_batch = lows[:, :, :adapter_rank_size].astype(jnp.bfloat16)
    low_out_b = lows[:, :, adapter_rank_size:].astype(jnp.bfloat16)

    adapter_grad = jnp.einsum(
        "bnr,brd->bnd", low_out_b, sel_down, preferred_element_type=jnp.float32
    )
    adapter_grad = adapter_grad.reshape(token_row_count, width_portion)
    grad_inputs = (base_grad + adapter_grad).astype(jnp.bfloat16)

    all_tenants = jnp.arange(tenant_number, dtype=jnp.int32)
    member = tenant_per_block[:, None] == all_tenants[None, :]
    member_b = member.astype(jnp.bfloat16)
    weighted_out = (member_b[:, None, :, None] * low_out_b[:, :, None, :]).reshape(
        token_row_count, tenant_number * adapter_rank_size
    )
    weighted_in = (member_b[:, None, :, None] * reduced_input_batch[:, :, None, :]).reshape(
        token_row_count, tenant_number * adapter_rank_size
    )
    down_contribution = lax.dot_general(
        weighted_out, inputs, (((0,), (0,)), ((), ())), preferred_element_type=jnp.float32
    )
    up_contribution = ADAPTER_SCALE * lax.dot_general(
        weighted_in, cotangent, (((0,), (0,)), ((), ())), preferred_element_type=jnp.float32
    )
    down_contribution = down_contribution.reshape(dp_size, held_tenants, adapter_rank_size, width_portion)
    up_contribution = up_contribution.reshape(dp_size, held_tenants, adapter_rank_size, key_portion)
    combined = jnp.concatenate([down_contribution, up_contribution], axis=3)
    owned = lax.dynamic_index_in_dim(combined, me_dp, 0, keepdims=False)
    for shift, pairs in _partners(dp_size):
        outgoing = lax.dynamic_index_in_dim(combined, _dest_of(me_dp, shift, dp_size), 0, keepdims=False)
        owned = owned + lax.ppermute(outgoing, "dp", pairs)
    grad_down = owned[:, :, :width_portion]
    grad_up = owned[:, :, width_portion:]
    return (grad_inputs, grad_down, grad_up)


def solution(mesh):
    in_specs = (
        P("dp", "tensor"),
        P("dp", "tensor"),
        P(None, "tensor"),
        P("dp", None, "tensor"),
        P("dp", None, "tensor"),
        P("dp"),
    )
    out_specs = (P("dp", "tensor"), P("dp", None, "tensor"), P("dp", None, "tensor"))
    return jax.shard_map(
        on_device, mesh=mesh, in_specs=in_specs, out_specs=out_specs, check_vma=False
    )
```

```python
import jax
import jax.numpy as jnp
from jax import lax
from jax.sharding import PartitionSpec as P

ADAPTER_SCALE = 2.0


def _partners(size):
    if size & (size - 1) == 0:
        return [(s, [(i, i ^ s) for i in range(size)]) for s in range(1, size)]
    return [(s, [(i, (i + s) % size) for i in range(size)]) for s in range(1, size)]


def _source_of(me, shift, size):
    if size & (size - 1) == 0:
        return me ^ shift
    return (me - shift + size) % size


def _dest_of(me, shift, size):
    if size & (size - 1) == 0:
        return me ^ shift
    return (me + shift) % size


def _gather_dp(local, axis, size):
    me = lax.axis_index(axis)
    got = [local]
    sources = [me]
    for shift, pairs in _partners(size):
        got.append(lax.ppermute(local, axis, pairs))
        sources.append(_source_of(me, shift, size))
    stacked = jnp.stack(got, 0)
    order = jnp.stack(sources)
    return stacked, order


def _psum_small(value, axis, size):
    total = value
    for _, pairs in _partners(size):
        total = total + lax.ppermute(value, axis, pairs)
    return total


def _frozen_term(cotangent, weight, axis, size):
    if size & (size - 1) != 0:
        partial = lax.dot_general(
            cotangent, weight, (((1,), (1,)), ((), ())), preferred_element_type=jnp.float32
        )
        return lax.psum_scatter(partial, axis, scatter_dimension=1, tiled=True)
    me = lax.axis_index(axis)
    rows = weight.shape[0] // size

    def term(block):
        piece = lax.dynamic_slice_in_dim(weight, block * rows, rows, axis=0)
        return lax.dot_general(
            cotangent, piece, (((1,), (1,)), ((), ())), preferred_element_type=jnp.float32
        )

    held = [term(me ^ e) for e in range(size)]
    step = 0
    while len(held) > 1:
        partner = 1 << step
        pairs = [(i, i ^ partner) for i in range(size)]
        got = [lax.ppermute(held[e], axis, pairs) for e in range(1, len(held), 2)]
        held = [held[e] + g for e, g in zip(range(0, len(held), 2), got)]
        step += 1
    return held[0]


def on_device(
    inputs, cotangent, frozen_key_weight, adapter_down_weight, adapter_up_weight, tenant_per_block
):
    token_row_count, width_portion = inputs.shape
    key_portion = cotangent.shape[1]
    block_count = tenant_per_block.shape[0]
    block_rows = token_row_count // block_count
    adapter_rank_size = adapter_down_weight.shape[1]
    held_tenants = adapter_down_weight.shape[0]
    dp_size = lax.axis_size("dp")
    tensor_size = lax.axis_size("tensor")
    tenant_number = dp_size * held_tenants
    me_dp = lax.axis_index("dp")

    base_grad = _frozen_term(cotangent, frozen_key_weight, "tensor", tensor_size)

    packed = jnp.concatenate([adapter_down_weight, adapter_up_weight], axis=2)
    stacked, order = _gather_dp(packed, "dp", dp_size)
    owner = tenant_per_block // held_tenants
    local = tenant_per_block % held_tenants
    pick = (order[None, :] == owner[:, None])
    pick = pick[:, :, None] & (jnp.arange(held_tenants)[None, None, :] == local[:, None, None])
    pick = pick.reshape(block_count, dp_size * held_tenants).astype(jnp.bfloat16)
    flat = stacked.reshape(dp_size * held_tenants, adapter_rank_size, width_portion + key_portion)
    selected = jnp.einsum("bk,krd->brd", pick, flat, preferred_element_type=jnp.float32).astype(jnp.bfloat16)
    sel_down = selected[:, :, :width_portion]
    sel_up = selected[:, :, width_portion:]

    input_blocks = inputs.reshape(block_count, block_rows, width_portion)
    cotangent_blocks = cotangent.reshape(block_count, block_rows, key_portion)
    low_in = jnp.einsum("bnd,brd->bnr", input_blocks, sel_down, preferred_element_type=jnp.float32)
    reduced_output = ADAPTER_SCALE * jnp.einsum(
        "bnk,brk->bnr", cotangent_blocks, sel_up, preferred_element_type=jnp.float32
    )
    lows = _psum_small(jnp.concatenate([low_in, reduced_output], axis=2), "tensor", tensor_size)
    reduced_input_batch = lows[:, :, :adapter_rank_size].astype(jnp.bfloat16)
    low_out_b = lows[:, :, adapter_rank_size:].astype(jnp.bfloat16)

    adapter_grad = jnp.einsum(
        "bnr,brd->bnd", low_out_b, sel_down, preferred_element_type=jnp.float32
    )
    adapter_grad = adapter_grad.reshape(token_row_count, width_portion)
    grad_inputs = (base_grad + adapter_grad).astype(jnp.bfloat16)

    all_tenants = jnp.arange(tenant_number, dtype=jnp.int32)
    member = tenant_per_block[:, None] == all_tenants[None, :]
    member_b = member.astype(jnp.bfloat16)
    weighted_out = (member_b[:, None, :, None] * low_out_b[:, :, None, :]).reshape(
        token_row_count, tenant_number * adapter_rank_size
    )
    weighted_in = (member_b[:, None, :, None] * reduced_input_batch[:, :, None, :]).reshape(
        token_row_count, tenant_number * adapter_rank_size
    )
    down_contribution = lax.dot_general(
        weighted_out, inputs, (((0,), (0,)), ((), ())), preferred_element_type=jnp.float32
    )
    up_contribution = ADAPTER_SCALE * lax.dot_general(
        weighted_in, cotangent, (((0,), (0,)), ((), ())), preferred_element_type=jnp.float32
    )
    down_contribution = down_contribution.reshape(dp_size, held_tenants, adapter_rank_size, width_portion)
    up_contribution = up_contribution.reshape(dp_size, held_tenants, adapter_rank_size, key_portion)
    combined = jnp.concatenate([down_contribution, up_contribution], axis=3)
    owned = lax.dynamic_index_in_dim(combined, me_dp, 0, keepdims=False)
    for shift, pairs in _partners(dp_size):
        outgoing = lax.dynamic_index_in_dim(combined, _dest_of(me_dp, shift, dp_size), 0, keepdims=False)
        owned = owned + lax.ppermute(outgoing.astype(jnp.bfloat16), "dp", pairs).astype(jnp.float32)
    grad_down = owned[:, :, :width_portion]
    grad_up = owned[:, :, width_portion:]
    return (grad_inputs, grad_down, grad_up)


def solution(mesh):
    in_specs = (
        P("dp", "tensor"),
        P("dp", "tensor"),
        P(None, "tensor"),
        P("dp", None, "tensor"),
        P("dp", None, "tensor"),
        P("dp"),
    )
    out_specs = (P("dp", "tensor"), P("dp", None, "tensor"), P("dp", None, "tensor"))
    return jax.shard_map(
        on_device, mesh=mesh, in_specs=in_specs, out_specs=out_specs, check_vma=False
    )
```

```python
import jax
import jax.numpy as jnp
from jax import lax
from jax.sharding import PartitionSpec as P

ADAPTER_SCALE = 2.0


def _partners(size):
    if size & (size - 1) == 0:
        return [(s, [(i, i ^ s) for i in range(size)]) for s in range(1, size)]
    return [(s, [(i, (i + s) % size) for i in range(size)]) for s in range(1, size)]


def _source_of(me, shift, size):
    if size & (size - 1) == 0:
        return me ^ shift
    return (me - shift + size) % size


def _dest_of(me, shift, size):
    if size & (size - 1) == 0:
        return me ^ shift
    return (me + shift) % size


def _gather_dp(local, axis, size):
    me = lax.axis_index(axis)
    got = [local]
    sources = [me]
    for shift, pairs in _partners(size):
        got.append(lax.ppermute(local, axis, pairs))
        sources.append(_source_of(me, shift, size))
    stacked = jnp.stack(got, 0)
    order = jnp.stack(sources)
    return stacked, order


def _psum_small(value, axis, size):
    total = value
    for _, pairs in _partners(size):
        total = total + lax.ppermute(value, axis, pairs)
    return total


def _frozen_term(cotangent, weight, axis, size):
    if size & (size - 1) != 0 or size == 1:
        partial = lax.dot_general(
            cotangent, weight, (((1,), (1,)), ((), ())), preferred_element_type=jnp.float32
        )
        return lax.psum_scatter(partial, axis, scatter_dimension=1, tiled=True)
    me = lax.axis_index(axis)
    rows = weight.shape[0] // size

    pairs = [(i, i ^ 1) for i in range(size)]
    pieces = [lax.dynamic_slice_in_dim(weight, (me ^ e) * rows, rows, axis=0) for e in range(size)]
    sent = jnp.stack(pieces[1::2], 0)
    their_rows = lax.ppermute(sent, axis, pairs)
    their_cot = lax.ppermute(cotangent, axis, pairs)

    def dot(a, b):
        return lax.dot_general(a, b, (((1,), (1,)), ((), ())), preferred_element_type=jnp.float32)

    held = [
        dot(cotangent, pieces[2 * m]) + dot(their_cot, their_rows[m])
        for m in range(size // 2)
    ]
    step = 1
    while len(held) > 1:
        partner = 1 << step
        pairs = [(i, i ^ partner) for i in range(size)]
        got = [lax.ppermute(held[e], axis, pairs) for e in range(1, len(held), 2)]
        held = [held[e] + g for e, g in zip(range(0, len(held), 2), got)]
        step += 1
    return held[0]


def on_device(
    inputs, cotangent, frozen_key_weight, adapter_down_weight, adapter_up_weight, tenant_per_block
):
    token_row_count, width_portion = inputs.shape
    key_portion = cotangent.shape[1]
    block_count = tenant_per_block.shape[0]
    block_rows = token_row_count // block_count
    adapter_rank_size = adapter_down_weight.shape[1]
    held_tenants = adapter_down_weight.shape[0]
    dp_size = lax.axis_size("dp")
    tensor_size = lax.axis_size("tensor")
    tenant_number = dp_size * held_tenants
    me_dp = lax.axis_index("dp")

    base_grad = _frozen_term(cotangent, frozen_key_weight, "tensor", tensor_size)

    packed = jnp.concatenate([adapter_down_weight, adapter_up_weight], axis=2)
    stacked, order = _gather_dp(packed, "dp", dp_size)
    owner = tenant_per_block // held_tenants
    local = tenant_per_block % held_tenants
    pick = (order[None, :] == owner[:, None])
    pick = pick[:, :, None] & (jnp.arange(held_tenants)[None, None, :] == local[:, None, None])
    pick = pick.reshape(block_count, dp_size * held_tenants).astype(jnp.bfloat16)
    flat = stacked.reshape(dp_size * held_tenants, adapter_rank_size, width_portion + key_portion)
    selected = jnp.einsum("bk,krd->brd", pick, flat, preferred_element_type=jnp.float32).astype(jnp.bfloat16)
    sel_down = selected[:, :, :width_portion]
    sel_up = selected[:, :, width_portion:]

    input_blocks = inputs.reshape(block_count, block_rows, width_portion)
    cotangent_blocks = cotangent.reshape(block_count, block_rows, key_portion)
    low_in = jnp.einsum("bnd,brd->bnr", input_blocks, sel_down, preferred_element_type=jnp.float32)
    reduced_output = ADAPTER_SCALE * jnp.einsum(
        "bnk,brk->bnr", cotangent_blocks, sel_up, preferred_element_type=jnp.float32
    )
    lows = _psum_small(jnp.concatenate([low_in, reduced_output], axis=2), "tensor", tensor_size)
    reduced_input_batch = lows[:, :, :adapter_rank_size].astype(jnp.bfloat16)
    low_out_b = lows[:, :, adapter_rank_size:].astype(jnp.bfloat16)

    adapter_grad = jnp.einsum(
        "bnr,brd->bnd", low_out_b, sel_down, preferred_element_type=jnp.float32
    )
    adapter_grad = adapter_grad.reshape(token_row_count, width_portion)
    grad_inputs = (base_grad + adapter_grad).astype(jnp.bfloat16)

    all_tenants = jnp.arange(tenant_number, dtype=jnp.int32)
    member = tenant_per_block[:, None] == all_tenants[None, :]
    member_b = member.astype(jnp.bfloat16)
    weighted_out = (member_b[:, None, :, None] * low_out_b[:, :, None, :]).reshape(
        token_row_count, tenant_number * adapter_rank_size
    )
    weighted_in = (member_b[:, None, :, None] * reduced_input_batch[:, :, None, :]).reshape(
        token_row_count, tenant_number * adapter_rank_size
    )
    down_contribution = lax.dot_general(
        weighted_out, inputs, (((0,), (0,)), ((), ())), preferred_element_type=jnp.float32
    )
    up_contribution = ADAPTER_SCALE * lax.dot_general(
        weighted_in, cotangent, (((0,), (0,)), ((), ())), preferred_element_type=jnp.float32
    )
    down_contribution = down_contribution.reshape(dp_size, held_tenants, adapter_rank_size, width_portion)
    up_contribution = up_contribution.reshape(dp_size, held_tenants, adapter_rank_size, key_portion)
    combined = jnp.concatenate([down_contribution, up_contribution], axis=3)
    owned = lax.dynamic_index_in_dim(combined, me_dp, 0, keepdims=False)
    for shift, pairs in _partners(dp_size):
        outgoing = lax.dynamic_index_in_dim(combined, _dest_of(me_dp, shift, dp_size), 0, keepdims=False)
        owned = owned + lax.ppermute(outgoing.astype(jnp.bfloat16), "dp", pairs).astype(jnp.float32)
    grad_down = owned[:, :, :width_portion]
    grad_up = owned[:, :, width_portion:]
    return (grad_inputs, grad_down, grad_up)


def solution(mesh):
    in_specs = (
        P("dp", "tensor"),
        P("dp", "tensor"),
        P(None, "tensor"),
        P("dp", None, "tensor"),
        P("dp", None, "tensor"),
        P("dp"),
    )
    out_specs = (P("dp", "tensor"), P("dp", None, "tensor"), P("dp", None, "tensor"))
    return jax.shard_map(
        on_device, mesh=mesh, in_specs=in_specs, out_specs=out_specs, check_vma=False
    )
```

```python
import jax
import jax.numpy as jnp
from jax import lax
from jax.sharding import PartitionSpec as P

ADAPTER_SCALE = 2.0


def _partners(size):
    if size & (size - 1) == 0:
        return [(s, [(i, i ^ s) for i in range(size)]) for s in range(1, size)]
    return [(s, [(i, (i + s) % size) for i in range(size)]) for s in range(1, size)]


def _source_of(me, shift, size):
    if size & (size - 1) == 0:
        return me ^ shift
    return (me - shift + size) % size


def _dest_of(me, shift, size):
    if size & (size - 1) == 0:
        return me ^ shift
    return (me + shift) % size


def _gather_dp(local, axis, size):
    me = lax.axis_index(axis)
    got = [local]
    sources = [me]
    for shift, pairs in _partners(size):
        got.append(lax.ppermute(local, axis, pairs))
        sources.append(_source_of(me, shift, size))
    stacked = jnp.stack(got, 0)
    order = jnp.stack(sources)
    return stacked, order


def _psum_small(value, axis, size):
    total = value
    for _, pairs in _partners(size):
        total = total + lax.ppermute(value, axis, pairs)
    return total


def _frozen_term(cotangent, weight, axis, size, ready=None):
    if size & (size - 1) != 0:
        partial = lax.dot_general(
            cotangent, weight, (((1,), (1,)), ((), ())), preferred_element_type=jnp.float32
        )
        return lax.psum_scatter(partial, axis, scatter_dimension=1, tiled=True), ready
    me = lax.axis_index(axis)
    rows = weight.shape[0] // size

    def term(block):
        piece = lax.dynamic_slice_in_dim(weight, block * rows, rows, axis=0)
        return lax.dot_general(
            cotangent, piece, (((1,), (1,)), ((), ())), preferred_element_type=jnp.float32
        )

    held = [term(me ^ e) for e in range(size)]
    step = 0
    while len(held) > 1:
        if step == 1 and ready is not None:
            *held, ready = lax.optimization_barrier((*held, ready))
        partner = 1 << step
        pairs = [(i, i ^ partner) for i in range(size)]
        got = [lax.ppermute(held[e], axis, pairs) for e in range(1, len(held), 2)]
        held = [held[e] + g for e, g in zip(range(0, len(held), 2), got)]
        step += 1
    return held[0], ready


def on_device(
    inputs, cotangent, frozen_key_weight, adapter_down_weight, adapter_up_weight, tenant_per_block
):
    token_row_count, width_portion = inputs.shape
    key_portion = cotangent.shape[1]
    block_count = tenant_per_block.shape[0]
    block_rows = token_row_count // block_count
    adapter_rank_size = adapter_down_weight.shape[1]
    held_tenants = adapter_down_weight.shape[0]
    dp_size = lax.axis_size("dp")
    tensor_size = lax.axis_size("tensor")
    tenant_number = dp_size * held_tenants
    me_dp = lax.axis_index("dp")


    packed = jnp.concatenate([adapter_down_weight, adapter_up_weight], axis=2)
    stacked, order = _gather_dp(packed, "dp", dp_size)
    owner = tenant_per_block // held_tenants
    local = tenant_per_block % held_tenants
    pick = (order[None, :] == owner[:, None])
    pick = pick[:, :, None] & (jnp.arange(held_tenants)[None, None, :] == local[:, None, None])
    pick = pick.reshape(block_count, dp_size * held_tenants).astype(jnp.bfloat16)
    flat = stacked.reshape(dp_size * held_tenants, adapter_rank_size, width_portion + key_portion)
    selected = jnp.einsum("bk,krd->brd", pick, flat, preferred_element_type=jnp.float32).astype(jnp.bfloat16)
    sel_down = selected[:, :, :width_portion]
    sel_up = selected[:, :, width_portion:]

    input_blocks = inputs.reshape(block_count, block_rows, width_portion)
    cotangent_blocks = cotangent.reshape(block_count, block_rows, key_portion)
    low_in = jnp.einsum("bnd,brd->bnr", input_blocks, sel_down, preferred_element_type=jnp.float32)
    reduced_output = ADAPTER_SCALE * jnp.einsum(
        "bnk,brk->bnr", cotangent_blocks, sel_up, preferred_element_type=jnp.float32
    )
    lows = jnp.concatenate([low_in, reduced_output], axis=2)
    base_grad, lows = _frozen_term(cotangent, frozen_key_weight, "tensor", tensor_size, lows)
    lows = _psum_small(lows, "tensor", tensor_size)
    reduced_input_batch = lows[:, :, :adapter_rank_size].astype(jnp.bfloat16)
    low_out_b = lows[:, :, adapter_rank_size:].astype(jnp.bfloat16)

    adapter_grad = jnp.einsum(
        "bnr,brd->bnd", low_out_b, sel_down, preferred_element_type=jnp.float32
    )
    adapter_grad = adapter_grad.reshape(token_row_count, width_portion)
    grad_inputs = (base_grad + adapter_grad).astype(jnp.bfloat16)

    all_tenants = jnp.arange(tenant_number, dtype=jnp.int32)
    member = tenant_per_block[:, None] == all_tenants[None, :]
    member_b = member.astype(jnp.bfloat16)
    weighted_out = (member_b[:, None, :, None] * low_out_b[:, :, None, :]).reshape(
        token_row_count, tenant_number * adapter_rank_size
    )
    weighted_in = (member_b[:, None, :, None] * reduced_input_batch[:, :, None, :]).reshape(
        token_row_count, tenant_number * adapter_rank_size
    )
    down_contribution = lax.dot_general(
        weighted_out, inputs, (((0,), (0,)), ((), ())), preferred_element_type=jnp.float32
    )
    up_contribution = ADAPTER_SCALE * lax.dot_general(
        weighted_in, cotangent, (((0,), (0,)), ((), ())), preferred_element_type=jnp.float32
    )
    down_contribution = down_contribution.reshape(dp_size, held_tenants, adapter_rank_size, width_portion)
    up_contribution = up_contribution.reshape(dp_size, held_tenants, adapter_rank_size, key_portion)
    combined = jnp.concatenate([down_contribution, up_contribution], axis=3)
    owned = lax.dynamic_index_in_dim(combined, me_dp, 0, keepdims=False)
    for shift, pairs in _partners(dp_size):
        outgoing = lax.dynamic_index_in_dim(combined, _dest_of(me_dp, shift, dp_size), 0, keepdims=False)
        owned = owned + lax.ppermute(outgoing.astype(jnp.bfloat16), "dp", pairs).astype(jnp.float32)
    grad_down = owned[:, :, :width_portion]
    grad_up = owned[:, :, width_portion:]
    return (grad_inputs, grad_down, grad_up)


def solution(mesh):
    in_specs = (
        P("dp", "tensor"),
        P("dp", "tensor"),
        P(None, "tensor"),
        P("dp", None, "tensor"),
        P("dp", None, "tensor"),
        P("dp"),
    )
    out_specs = (P("dp", "tensor"), P("dp", None, "tensor"), P("dp", None, "tensor"))
    return jax.shard_map(
        on_device, mesh=mesh, in_specs=in_specs, out_specs=out_specs, check_vma=False
    )
```

```python
import jax
import jax.numpy as jnp
from jax import lax
from jax.sharding import PartitionSpec as P

ADAPTER_SCALE = 2.0


def _partners(size):
    if size & (size - 1) == 0:
        return [(s, [(i, i ^ s) for i in range(size)]) for s in range(1, size)]
    return [(s, [(i, (i + s) % size) for i in range(size)]) for s in range(1, size)]


def _source_of(me, shift, size):
    if size & (size - 1) == 0:
        return me ^ shift
    return (me - shift + size) % size


def _dest_of(me, shift, size):
    if size & (size - 1) == 0:
        return me ^ shift
    return (me + shift) % size


def _gather_dp(local, axis, size):
    me = lax.axis_index(axis)
    got = [local]
    sources = [me]
    for shift, pairs in _partners(size):
        got.append(lax.ppermute(local, axis, pairs))
        sources.append(_source_of(me, shift, size))
    stacked = jnp.stack(got, 0)
    order = jnp.stack(sources)
    return stacked, order


def _psum_small(value, axis, size):
    if size & (size - 1) != 0:
        total = value
        for _, pairs in _partners(size):
            total = total + lax.ppermute(value, axis, pairs)
        return total
    total = value
    step = 1
    while step < size:
        total = total + lax.ppermute(total, axis, [(i, i ^ step) for i in range(size)])
        step *= 2
    return total


def _frozen_term(cotangent, weight, axis, size, ready=None):
    if size & (size - 1) != 0:
        partial = lax.dot_general(
            cotangent, weight, (((1,), (1,)), ((), ())), preferred_element_type=jnp.float32
        )
        return lax.psum_scatter(partial, axis, scatter_dimension=1, tiled=True), ready
    me = lax.axis_index(axis)
    rows = weight.shape[0] // size

    def term(block):
        piece = lax.dynamic_slice_in_dim(weight, block * rows, rows, axis=0)
        return lax.dot_general(
            cotangent, piece, (((1,), (1,)), ((), ())), preferred_element_type=jnp.float32
        )

    held = [term(me ^ e) for e in range(size)]
    step = 0
    while len(held) > 1:
        if step == 1 and ready is not None:
            *leaving, ready = lax.optimization_barrier((*held[1::2], ready))
            held[1::2] = leaving
        partner = 1 << step
        pairs = [(i, i ^ partner) for i in range(size)]
        got = [lax.ppermute(held[e], axis, pairs) for e in range(1, len(held), 2)]
        held = [held[e] + g for e, g in zip(range(0, len(held), 2), got)]
        step += 1
    return held[0], ready


def on_device(
    inputs, cotangent, frozen_key_weight, adapter_down_weight, adapter_up_weight, tenant_per_block
):
    token_row_count, width_portion = inputs.shape
    key_portion = cotangent.shape[1]
    block_count = tenant_per_block.shape[0]
    block_rows = token_row_count // block_count
    adapter_rank_size = adapter_down_weight.shape[1]
    held_tenants = adapter_down_weight.shape[0]
    dp_size = lax.axis_size("dp")
    tensor_size = lax.axis_size("tensor")
    tenant_number = dp_size * held_tenants
    me_dp = lax.axis_index("dp")


    packed = jnp.concatenate([adapter_down_weight, adapter_up_weight], axis=2)
    stacked, order = _gather_dp(packed, "dp", dp_size)
    owner = tenant_per_block // held_tenants
    local = tenant_per_block % held_tenants
    pick = (order[None, :] == owner[:, None])
    pick = pick[:, :, None] & (jnp.arange(held_tenants)[None, None, :] == local[:, None, None])
    pick = pick.reshape(block_count, dp_size * held_tenants).astype(jnp.bfloat16)
    flat = stacked.reshape(dp_size * held_tenants, adapter_rank_size, width_portion + key_portion)
    selected = jnp.einsum("bk,krd->brd", pick, flat, preferred_element_type=jnp.float32).astype(jnp.bfloat16)
    sel_down = selected[:, :, :width_portion]
    sel_up = selected[:, :, width_portion:]

    input_blocks = inputs.reshape(block_count, block_rows, width_portion)
    cotangent_blocks = cotangent.reshape(block_count, block_rows, key_portion)
    low_in = jnp.einsum("bnd,brd->bnr", input_blocks, sel_down, preferred_element_type=jnp.float32)
    reduced_output = ADAPTER_SCALE * jnp.einsum(
        "bnk,brk->bnr", cotangent_blocks, sel_up, preferred_element_type=jnp.float32
    )
    lows = jnp.concatenate([low_in, reduced_output], axis=2)
    base_grad, lows = _frozen_term(cotangent, frozen_key_weight, "tensor", tensor_size, lows)
    lows = _psum_small(lows, "tensor", tensor_size)
    reduced_input_batch = lows[:, :, :adapter_rank_size].astype(jnp.bfloat16)
    low_out_b = lows[:, :, adapter_rank_size:].astype(jnp.bfloat16)

    adapter_grad = jnp.einsum(
        "bnr,brd->bnd", low_out_b, sel_down, preferred_element_type=jnp.float32
    )
    adapter_grad = adapter_grad.reshape(token_row_count, width_portion)
    grad_inputs = (base_grad + adapter_grad).astype(jnp.bfloat16)

    all_tenants = jnp.arange(tenant_number, dtype=jnp.int32)
    member = tenant_per_block[:, None] == all_tenants[None, :]
    member_b = member.astype(jnp.bfloat16)
    weighted_out = (member_b[:, None, :, None] * low_out_b[:, :, None, :]).reshape(
        token_row_count, tenant_number * adapter_rank_size
    )
    weighted_in = (member_b[:, None, :, None] * reduced_input_batch[:, :, None, :]).reshape(
        token_row_count, tenant_number * adapter_rank_size
    )
    down_contribution = lax.dot_general(
        weighted_out, inputs, (((0,), (0,)), ((), ())), preferred_element_type=jnp.float32
    )
    up_contribution = ADAPTER_SCALE * lax.dot_general(
        weighted_in, cotangent, (((0,), (0,)), ((), ())), preferred_element_type=jnp.float32
    )
    down_contribution = down_contribution.reshape(dp_size, held_tenants, adapter_rank_size, width_portion)
    up_contribution = up_contribution.reshape(dp_size, held_tenants, adapter_rank_size, key_portion)
    combined = jnp.concatenate([down_contribution, up_contribution], axis=3)
    owned = lax.dynamic_index_in_dim(combined, me_dp, 0, keepdims=False)
    for shift, pairs in _partners(dp_size):
        outgoing = lax.dynamic_index_in_dim(combined, _dest_of(me_dp, shift, dp_size), 0, keepdims=False)
        owned = owned + lax.ppermute(outgoing.astype(jnp.bfloat16), "dp", pairs).astype(jnp.float32)
    grad_down = owned[:, :, :width_portion]
    grad_up = owned[:, :, width_portion:]
    return (grad_inputs, grad_down, grad_up)


def solution(mesh):
    in_specs = (
        P("dp", "tensor"),
        P("dp", "tensor"),
        P(None, "tensor"),
        P("dp", None, "tensor"),
        P("dp", None, "tensor"),
        P("dp"),
    )
    out_specs = (P("dp", "tensor"), P("dp", None, "tensor"), P("dp", None, "tensor"))
    return jax.shard_map(
        on_device, mesh=mesh, in_specs=in_specs, out_specs=out_specs, check_vma=False
    )
```

```python
import jax
import jax.numpy as jnp
from jax import lax
from jax.sharding import PartitionSpec as P

ADAPTER_SCALE = 2.0


def _partners(size):
    if size & (size - 1) == 0:
        return [(s, [(i, i ^ s) for i in range(size)]) for s in range(1, size)]
    return [(s, [(i, (i + s) % size) for i in range(size)]) for s in range(1, size)]


def _source_of(me, shift, size):
    if size & (size - 1) == 0:
        return me ^ shift
    return (me - shift + size) % size


def _dest_of(me, shift, size):
    if size & (size - 1) == 0:
        return me ^ shift
    return (me + shift) % size


def _gather_dp(local, axis, size):
    me = lax.axis_index(axis)
    if size & (size - 1) != 0 or size < 4:
        got = [local]
        sources = [me]
        for shift, pairs in _partners(size):
            got.append(lax.ppermute(local, axis, pairs))
            sources.append(_source_of(me, shift, size))
        return jnp.stack(got, 0), jnp.stack(sources)
    pair = jnp.concatenate([local, lax.ppermute(local, axis, [(i, i ^ 1) for i in range(size)])], 0)
    got = [pair]
    sources = [me, me ^ 1]
    for m in range(1, size // 2):
        shift = 2 * m
        got.append(lax.ppermute(pair, axis, [(i, i ^ shift) for i in range(size)]))
        sources += [me ^ shift, me ^ shift ^ 1]
    return jnp.concatenate(got, 0), jnp.stack(sources)


def _psum_small(value, axis, size):
    if size & (size - 1) != 0:
        total = value
        for _, pairs in _partners(size):
            total = total + lax.ppermute(value, axis, pairs)
        return total
    total = value
    step = 1
    while step < size:
        total = total + lax.ppermute(total, axis, [(i, i ^ step) for i in range(size)])
        step *= 2
    return total


def _frozen_term(cotangent, weight, axis, size, ready=None):
    if size & (size - 1) != 0:
        partial = lax.dot_general(
            cotangent, weight, (((1,), (1,)), ((), ())), preferred_element_type=jnp.float32
        )
        return lax.psum_scatter(partial, axis, scatter_dimension=1, tiled=True), ready
    me = lax.axis_index(axis)
    rows = weight.shape[0] // size

    def term(block):
        piece = lax.dynamic_slice_in_dim(weight, block * rows, rows, axis=0)
        return lax.dot_general(
            cotangent, piece, (((1,), (1,)), ((), ())), preferred_element_type=jnp.float32
        )

    held = [term(me ^ e) for e in range(size)]
    step = 0
    while len(held) > 1:
        if step == 1 and ready is not None:
            *leaving, ready = lax.optimization_barrier((*held[1::2], ready))
            held[1::2] = leaving
        partner = 1 << step
        pairs = [(i, i ^ partner) for i in range(size)]
        got = [lax.ppermute(held[e], axis, pairs) for e in range(1, len(held), 2)]
        held = [held[e] + g for e, g in zip(range(0, len(held), 2), got)]
        step += 1
    return held[0], ready


def on_device(
    inputs, cotangent, frozen_key_weight, adapter_down_weight, adapter_up_weight, tenant_per_block
):
    token_row_count, width_portion = inputs.shape
    key_portion = cotangent.shape[1]
    block_count = tenant_per_block.shape[0]
    block_rows = token_row_count // block_count
    adapter_rank_size = adapter_down_weight.shape[1]
    held_tenants = adapter_down_weight.shape[0]
    dp_size = lax.axis_size("dp")
    tensor_size = lax.axis_size("tensor")
    tenant_number = dp_size * held_tenants
    me_dp = lax.axis_index("dp")


    packed = jnp.concatenate([adapter_down_weight, adapter_up_weight], axis=2)
    stacked, order = _gather_dp(packed, "dp", dp_size)
    stacked = stacked.reshape(dp_size, held_tenants, *packed.shape[1:])
    owner = tenant_per_block // held_tenants
    local = tenant_per_block % held_tenants
    pick = (order[None, :] == owner[:, None])
    pick = pick[:, :, None] & (jnp.arange(held_tenants)[None, None, :] == local[:, None, None])
    pick = pick.reshape(block_count, dp_size * held_tenants).astype(jnp.bfloat16)
    flat = stacked.reshape(dp_size * held_tenants, adapter_rank_size, width_portion + key_portion)
    selected = jnp.einsum("bk,krd->brd", pick, flat, preferred_element_type=jnp.float32).astype(jnp.bfloat16)
    sel_down = selected[:, :, :width_portion]
    sel_up = selected[:, :, width_portion:]

    input_blocks = inputs.reshape(block_count, block_rows, width_portion)
    cotangent_blocks = cotangent.reshape(block_count, block_rows, key_portion)
    low_in = jnp.einsum("bnd,brd->bnr", input_blocks, sel_down, preferred_element_type=jnp.float32)
    reduced_output = ADAPTER_SCALE * jnp.einsum(
        "bnk,brk->bnr", cotangent_blocks, sel_up, preferred_element_type=jnp.float32
    )
    lows = jnp.concatenate([low_in, reduced_output], axis=2)
    base_grad, lows = _frozen_term(cotangent, frozen_key_weight, "tensor", tensor_size, lows)
    lows = _psum_small(lows, "tensor", tensor_size)
    reduced_input_batch = lows[:, :, :adapter_rank_size].astype(jnp.bfloat16)
    low_out_b = lows[:, :, adapter_rank_size:].astype(jnp.bfloat16)

    adapter_grad = jnp.einsum(
        "bnr,brd->bnd", low_out_b, sel_down, preferred_element_type=jnp.float32
    )
    adapter_grad = adapter_grad.reshape(token_row_count, width_portion)
    grad_inputs = (base_grad + adapter_grad).astype(jnp.bfloat16)

    all_tenants = jnp.arange(tenant_number, dtype=jnp.int32)
    member = tenant_per_block[:, None] == all_tenants[None, :]
    member_b = member.astype(jnp.bfloat16)
    weighted_out = (member_b[:, None, :, None] * low_out_b[:, :, None, :]).reshape(
        token_row_count, tenant_number * adapter_rank_size
    )
    weighted_in = (member_b[:, None, :, None] * reduced_input_batch[:, :, None, :]).reshape(
        token_row_count, tenant_number * adapter_rank_size
    )
    down_contribution = lax.dot_general(
        weighted_out, inputs, (((0,), (0,)), ((), ())), preferred_element_type=jnp.float32
    )
    up_contribution = ADAPTER_SCALE * lax.dot_general(
        weighted_in, cotangent, (((0,), (0,)), ((), ())), preferred_element_type=jnp.float32
    )
    down_contribution = down_contribution.reshape(dp_size, held_tenants, adapter_rank_size, width_portion)
    up_contribution = up_contribution.reshape(dp_size, held_tenants, adapter_rank_size, key_portion)
    combined = jnp.concatenate([down_contribution, up_contribution], axis=3)
    owned = lax.dynamic_index_in_dim(combined, me_dp, 0, keepdims=False)
    grad_down = owned[:, :, :width_portion]
    grad_up = owned[:, :, width_portion:]
    for shift, pairs in _partners(dp_size):
        outgoing = lax.dynamic_index_in_dim(combined, _dest_of(me_dp, shift, dp_size), 0, keepdims=False)
        arrived = lax.ppermute(outgoing.astype(jnp.bfloat16), "dp", pairs).astype(jnp.float32)
        grad_down = grad_down + arrived[:, :, :width_portion]
        grad_up = grad_up + arrived[:, :, width_portion:]
    return (grad_inputs, grad_down, grad_up)


def solution(mesh):
    in_specs = (
        P("dp", "tensor"),
        P("dp", "tensor"),
        P(None, "tensor"),
        P("dp", None, "tensor"),
        P("dp", None, "tensor"),
        P("dp"),
    )
    out_specs = (P("dp", "tensor"), P("dp", None, "tensor"), P("dp", None, "tensor"))
    return jax.shard_map(
        on_device, mesh=mesh, in_specs=in_specs, out_specs=out_specs, check_vma=False
    )
```

```python
import jax
import jax.numpy as jnp
from jax import lax
from jax.sharding import PartitionSpec as P

ADAPTER_SCALE = 2.0


def _partners(size):
    if size & (size - 1) == 0:
        return [(s, [(i, i ^ s) for i in range(size)]) for s in range(1, size)]
    return [(s, [(i, (i + s) % size) for i in range(size)]) for s in range(1, size)]


def _source_of(me, shift, size):
    if size & (size - 1) == 0:
        return me ^ shift
    return (me - shift + size) % size


def _dest_of(me, shift, size):
    if size & (size - 1) == 0:
        return me ^ shift
    return (me + shift) % size


def _gather_dp(local, axis, size):
    me = lax.axis_index(axis)
    if size & (size - 1) != 0 or size < 4:
        got = [local]
        sources = [me]
        for shift, pairs in _partners(size):
            got.append(lax.ppermute(local, axis, pairs))
            sources.append(_source_of(me, shift, size))
        return jnp.stack(got, 0), jnp.stack(sources)
    pair = jnp.concatenate([local, lax.ppermute(local, axis, [(i, i ^ 1) for i in range(size)])], 0)
    got = [pair]
    sources = [me, me ^ 1]
    for m in range(1, size // 2):
        shift = 2 * m
        got.append(lax.ppermute(pair, axis, [(i, i ^ shift) for i in range(size)]))
        sources += [me ^ shift, me ^ shift ^ 1]
    return jnp.concatenate(got, 0), jnp.stack(sources)


def _psum_small(value, axis, size):
    if size & (size - 1) != 0:
        total = value
        for _, pairs in _partners(size):
            total = total + lax.ppermute(value, axis, pairs)
        return total
    total = value
    step = 1
    while step < size:
        total = total + lax.ppermute(total, axis, [(i, i ^ step) for i in range(size)])
        step *= 2
    return total


def _frozen_terms(cotangent, weight, axis, size):
    me = lax.axis_index(axis)
    rows = weight.shape[0] // size

    def term(block):
        piece = lax.dynamic_slice_in_dim(weight, block * rows, rows, axis=0)
        return lax.dot_general(
            cotangent, piece, (((1,), (1,)), ((), ())), preferred_element_type=jnp.float32
        )

    return [term(me ^ e) for e in range(size)]


def _frozen_reduce(held, axis, size, ready):
    step = 0
    while len(held) > 1:
        if step == 1:
            *leaving, ready = lax.optimization_barrier((*held[1::2], ready))
            held[1::2] = leaving
        partner = 1 << step
        pairs = [(i, i ^ partner) for i in range(size)]
        got = [lax.ppermute(held[e], axis, pairs) for e in range(1, len(held), 2)]
        held = [held[e] + g for e, g in zip(range(0, len(held), 2), got)]
        step += 1
    return held[0], ready


def on_device(
    inputs, cotangent, frozen_key_weight, adapter_down_weight, adapter_up_weight, tenant_per_block
):
    token_row_count, width_portion = inputs.shape
    key_portion = cotangent.shape[1]
    block_count = tenant_per_block.shape[0]
    block_rows = token_row_count // block_count
    adapter_rank_size = adapter_down_weight.shape[1]
    held_tenants = adapter_down_weight.shape[0]
    dp_size = lax.axis_size("dp")
    tensor_size = lax.axis_size("tensor")
    tenant_number = dp_size * held_tenants
    me_dp = lax.axis_index("dp")


    packed = jnp.concatenate([adapter_down_weight, adapter_up_weight], axis=2)
    halving = tensor_size > 1 and tensor_size & (tensor_size - 1) == 0
    if halving:
        frozen = _frozen_terms(cotangent, frozen_key_weight, "tensor", tensor_size)
        *leaving, packed = lax.optimization_barrier((*frozen[1::2], packed))
        frozen[1::2] = leaving
    stacked, order = _gather_dp(packed, "dp", dp_size)
    stacked = stacked.reshape(dp_size, held_tenants, *packed.shape[1:])
    owner = tenant_per_block // held_tenants
    local = tenant_per_block % held_tenants
    pick = (order[None, :] == owner[:, None])
    pick = pick[:, :, None] & (jnp.arange(held_tenants)[None, None, :] == local[:, None, None])
    pick = pick.reshape(block_count, dp_size * held_tenants).astype(jnp.bfloat16)
    flat = stacked.reshape(dp_size * held_tenants, adapter_rank_size, width_portion + key_portion)
    selected = jnp.einsum("bk,krd->brd", pick, flat, preferred_element_type=jnp.float32).astype(jnp.bfloat16)
    sel_down = selected[:, :, :width_portion]
    sel_up = selected[:, :, width_portion:]

    input_blocks = inputs.reshape(block_count, block_rows, width_portion)
    cotangent_blocks = cotangent.reshape(block_count, block_rows, key_portion)
    low_in = jnp.einsum("bnd,brd->bnr", input_blocks, sel_down, preferred_element_type=jnp.float32)
    reduced_output = ADAPTER_SCALE * jnp.einsum(
        "bnk,brk->bnr", cotangent_blocks, sel_up, preferred_element_type=jnp.float32
    )
    lows = jnp.concatenate([low_in, reduced_output], axis=2)
    if halving:
        base_grad, lows = _frozen_reduce(frozen, "tensor", tensor_size, lows)
    else:
        partial = lax.dot_general(
            cotangent, frozen_key_weight, (((1,), (1,)), ((), ())), preferred_element_type=jnp.float32
        )
        base_grad = lax.psum_scatter(partial, "tensor", scatter_dimension=1, tiled=True)
    lows = _psum_small(lows, "tensor", tensor_size)
    reduced_input_batch = lows[:, :, :adapter_rank_size].astype(jnp.bfloat16)
    low_out_b = lows[:, :, adapter_rank_size:].astype(jnp.bfloat16)

    adapter_grad = jnp.einsum(
        "bnr,brd->bnd", low_out_b, sel_down, preferred_element_type=jnp.float32
    )
    adapter_grad = adapter_grad.reshape(token_row_count, width_portion)
    grad_inputs = (base_grad + adapter_grad).astype(jnp.bfloat16)

    all_tenants = jnp.arange(tenant_number, dtype=jnp.int32)
    member = tenant_per_block[:, None] == all_tenants[None, :]
    member_b = member.astype(jnp.bfloat16)
    weighted_out = (member_b[:, None, :, None] * low_out_b[:, :, None, :]).reshape(
        token_row_count, tenant_number * adapter_rank_size
    )
    weighted_in = (member_b[:, None, :, None] * reduced_input_batch[:, :, None, :]).reshape(
        token_row_count, tenant_number * adapter_rank_size
    )
    down_contribution = lax.dot_general(
        weighted_out, inputs, (((0,), (0,)), ((), ())), preferred_element_type=jnp.float32
    )
    up_contribution = ADAPTER_SCALE * lax.dot_general(
        weighted_in, cotangent, (((0,), (0,)), ((), ())), preferred_element_type=jnp.float32
    )
    down_contribution = down_contribution.reshape(dp_size, held_tenants, adapter_rank_size, width_portion)
    up_contribution = up_contribution.reshape(dp_size, held_tenants, adapter_rank_size, key_portion)
    combined = jnp.concatenate([down_contribution, up_contribution], axis=3)
    owned = lax.dynamic_index_in_dim(combined, me_dp, 0, keepdims=False)
    grad_down = owned[:, :, :width_portion]
    grad_up = owned[:, :, width_portion:]
    for shift, pairs in _partners(dp_size):
        outgoing = lax.dynamic_index_in_dim(combined, _dest_of(me_dp, shift, dp_size), 0, keepdims=False)
        arrived = lax.ppermute(outgoing.astype(jnp.bfloat16), "dp", pairs).astype(jnp.float32)
        grad_down = grad_down + arrived[:, :, :width_portion]
        grad_up = grad_up + arrived[:, :, width_portion:]
    return (grad_inputs, grad_down, grad_up)


def solution(mesh):
    in_specs = (
        P("dp", "tensor"),
        P("dp", "tensor"),
        P(None, "tensor"),
        P("dp", None, "tensor"),
        P("dp", None, "tensor"),
        P("dp"),
    )
    out_specs = (P("dp", "tensor"), P("dp", None, "tensor"), P("dp", None, "tensor"))
    return jax.shard_map(
        on_device, mesh=mesh, in_specs=in_specs, out_specs=out_specs, check_vma=False
    )
```

```python
import jax
import jax.numpy as jnp
from jax import lax
from jax.sharding import PartitionSpec as P

ADAPTER_SCALE = 2.0


def _partners(size):
    if size & (size - 1) == 0:
        return [(s, [(i, i ^ s) for i in range(size)]) for s in range(1, size)]
    return [(s, [(i, (i + s) % size) for i in range(size)]) for s in range(1, size)]


def _source_of(me, shift, size):
    if size & (size - 1) == 0:
        return me ^ shift
    return (me - shift + size) % size


def _dest_of(me, shift, size):
    if size & (size - 1) == 0:
        return me ^ shift
    return (me + shift) % size


def _gather_dp(local, axis, size):
    me = lax.axis_index(axis)
    if size & (size - 1) != 0 or size < 4:
        got = [local]
        sources = [me]
        for shift, pairs in _partners(size):
            got.append(lax.ppermute(local, axis, pairs))
            sources.append(_source_of(me, shift, size))
        return jnp.stack(got, 0), jnp.stack(sources)
    pair = jnp.concatenate([local, lax.ppermute(local, axis, [(i, i ^ 1) for i in range(size)])], 0)
    got = [pair]
    sources = [me, me ^ 1]
    for m in range(1, size // 2):
        shift = 2 * m
        got.append(lax.ppermute(pair, axis, [(i, i ^ shift) for i in range(size)]))
        sources += [me ^ shift, me ^ shift ^ 1]
    return jnp.concatenate(got, 0), jnp.stack(sources)


def _psum_small(value, axis, size):
    if size & (size - 1) != 0:
        total = value
        for _, pairs in _partners(size):
            total = total + lax.ppermute(value, axis, pairs)
        return total
    total = value
    step = 1
    while step < size:
        total = total + lax.ppermute(total, axis, [(i, i ^ step) for i in range(size)])
        step *= 2
    return total


def _frozen_term(cotangent, weight, axis, size, ready=None):
    if size & (size - 1) != 0:
        partial = lax.dot_general(
            cotangent, weight, (((1,), (1,)), ((), ())), preferred_element_type=jnp.float32
        )
        return lax.psum_scatter(partial, axis, scatter_dimension=1, tiled=True), ready
    me = lax.axis_index(axis)
    rows = weight.shape[0] // size

    def term(block):
        piece = lax.dynamic_slice_in_dim(weight, block * rows, rows, axis=0)
        return lax.dot_general(
            cotangent, piece, (((1,), (1,)), ((), ())), preferred_element_type=jnp.float32
        )

    pieces = [lax.dynamic_slice_in_dim(weight, (me ^ e) * rows, rows, axis=0) for e in range(1, size, 2)]
    leaving = jnp.einsum(
        "nk,bdk->bnd", cotangent, jnp.stack(pieces, 0), preferred_element_type=jnp.float32
    )
    pairs = [(i, i ^ 1) for i in range(size)]
    got = lax.ppermute(leaving, axis, pairs)
    held = [term(me ^ e) + got[m] for m, e in enumerate(range(0, size, 2))]
    step = 1
    while len(held) > 1:
        if step == 1 and ready is not None:
            *leaving, ready = lax.optimization_barrier((*held[1::2], ready))
            held[1::2] = leaving
        partner = 1 << step
        pairs = [(i, i ^ partner) for i in range(size)]
        got = [lax.ppermute(held[e], axis, pairs) for e in range(1, len(held), 2)]
        held = [held[e] + g for e, g in zip(range(0, len(held), 2), got)]
        step += 1
    return held[0], ready


def on_device(
    inputs, cotangent, frozen_key_weight, adapter_down_weight, adapter_up_weight, tenant_per_block
):
    token_row_count, width_portion = inputs.shape
    key_portion = cotangent.shape[1]
    block_count = tenant_per_block.shape[0]
    block_rows = token_row_count // block_count
    adapter_rank_size = adapter_down_weight.shape[1]
    held_tenants = adapter_down_weight.shape[0]
    dp_size = lax.axis_size("dp")
    tensor_size = lax.axis_size("tensor")
    tenant_number = dp_size * held_tenants
    me_dp = lax.axis_index("dp")


    packed = jnp.concatenate([adapter_down_weight, adapter_up_weight], axis=2)
    stacked, order = _gather_dp(packed, "dp", dp_size)
    stacked = stacked.reshape(dp_size, held_tenants, *packed.shape[1:])
    owner = tenant_per_block // held_tenants
    local = tenant_per_block % held_tenants
    pick = (order[None, :] == owner[:, None])
    pick = pick[:, :, None] & (jnp.arange(held_tenants)[None, None, :] == local[:, None, None])
    pick = pick.reshape(block_count, dp_size * held_tenants).astype(jnp.bfloat16)
    flat = stacked.reshape(dp_size * held_tenants, adapter_rank_size, width_portion + key_portion)
    selected = jnp.einsum("bk,krd->brd", pick, flat, preferred_element_type=jnp.float32).astype(jnp.bfloat16)
    sel_down = selected[:, :, :width_portion]
    sel_up = selected[:, :, width_portion:]

    input_blocks = inputs.reshape(block_count, block_rows, width_portion)
    cotangent_blocks = cotangent.reshape(block_count, block_rows, key_portion)
    low_in = jnp.einsum("bnd,brd->bnr", input_blocks, sel_down, preferred_element_type=jnp.float32)
    reduced_output = ADAPTER_SCALE * jnp.einsum(
        "bnk,brk->bnr", cotangent_blocks, sel_up, preferred_element_type=jnp.float32
    )
    lows = jnp.concatenate([low_in, reduced_output], axis=2)
    base_grad, lows = _frozen_term(cotangent, frozen_key_weight, "tensor", tensor_size, lows)
    lows = _psum_small(lows, "tensor", tensor_size)
    reduced_input_batch = lows[:, :, :adapter_rank_size].astype(jnp.bfloat16)
    low_out_b = lows[:, :, adapter_rank_size:].astype(jnp.bfloat16)

    adapter_grad = jnp.einsum(
        "bnr,brd->bnd", low_out_b, sel_down, preferred_element_type=jnp.float32
    )
    adapter_grad = adapter_grad.reshape(token_row_count, width_portion)
    grad_inputs = (base_grad + adapter_grad).astype(jnp.bfloat16)

    all_tenants = jnp.arange(tenant_number, dtype=jnp.int32)
    member = tenant_per_block[:, None] == all_tenants[None, :]
    member_b = member.astype(jnp.bfloat16)
    weighted_out = (member_b[:, None, :, None] * low_out_b[:, :, None, :]).reshape(
        token_row_count, tenant_number * adapter_rank_size
    )
    weighted_in = (member_b[:, None, :, None] * reduced_input_batch[:, :, None, :]).reshape(
        token_row_count, tenant_number * adapter_rank_size
    )
    down_contribution = lax.dot_general(
        weighted_out, inputs, (((0,), (0,)), ((), ())), preferred_element_type=jnp.float32
    )
    up_contribution = ADAPTER_SCALE * lax.dot_general(
        weighted_in, cotangent, (((0,), (0,)), ((), ())), preferred_element_type=jnp.float32
    )
    down_contribution = down_contribution.reshape(dp_size, held_tenants, adapter_rank_size, width_portion)
    up_contribution = up_contribution.reshape(dp_size, held_tenants, adapter_rank_size, key_portion)
    combined = jnp.concatenate([down_contribution, up_contribution], axis=3)
    owned = lax.dynamic_index_in_dim(combined, me_dp, 0, keepdims=False)
    grad_down = owned[:, :, :width_portion]
    grad_up = owned[:, :, width_portion:]
    for shift, pairs in _partners(dp_size):
        outgoing = lax.dynamic_index_in_dim(combined, _dest_of(me_dp, shift, dp_size), 0, keepdims=False)
        arrived = lax.ppermute(outgoing.astype(jnp.bfloat16), "dp", pairs).astype(jnp.float32)
        grad_down = grad_down + arrived[:, :, :width_portion]
        grad_up = grad_up + arrived[:, :, width_portion:]
    return (grad_inputs, grad_down, grad_up)


def solution(mesh):
    in_specs = (
        P("dp", "tensor"),
        P("dp", "tensor"),
        P(None, "tensor"),
        P("dp", None, "tensor"),
        P("dp", None, "tensor"),
        P("dp"),
    )
    out_specs = (P("dp", "tensor"), P("dp", None, "tensor"), P("dp", None, "tensor"))
    return jax.shard_map(
        on_device, mesh=mesh, in_specs=in_specs, out_specs=out_specs, check_vma=False
    )
```

```python
import jax
import jax.numpy as jnp
from jax import lax
from jax.sharding import PartitionSpec as P

ADAPTER_SCALE = 2.0


def _partners(size):
    if size & (size - 1) == 0:
        return [(s, [(i, i ^ s) for i in range(size)]) for s in range(1, size)]
    return [(s, [(i, (i + s) % size) for i in range(size)]) for s in range(1, size)]


def _source_of(me, shift, size):
    if size & (size - 1) == 0:
        return me ^ shift
    return (me - shift + size) % size


def _dest_of(me, shift, size):
    if size & (size - 1) == 0:
        return me ^ shift
    return (me + shift) % size


def _gather_dp(local, axis, size):
    me = lax.axis_index(axis)
    if size & (size - 1) != 0 or size < 4:
        got = [local]
        sources = [me]
        for shift, pairs in _partners(size):
            got.append(lax.ppermute(local, axis, pairs))
            sources.append(_source_of(me, shift, size))
        return jnp.stack(got, 0), jnp.stack(sources)
    pair = jnp.concatenate([local, lax.ppermute(local, axis, [(i, i ^ 1) for i in range(size)])], 0)
    got = [pair]
    sources = [me, me ^ 1]
    for m in range(1, size // 2):
        shift = 2 * m
        got.append(lax.ppermute(pair, axis, [(i, i ^ shift) for i in range(size)]))
        sources += [me ^ shift, me ^ shift ^ 1]
    return jnp.concatenate(got, 0), jnp.stack(sources)


def _psum_small(value, axis, size):
    if size & (size - 1) != 0:
        total = value
        for _, pairs in _partners(size):
            total = total + lax.ppermute(value, axis, pairs)
        return total
    total = value
    step = 1
    while step < size:
        total = total + lax.ppermute(total, axis, [(i, i ^ step) for i in range(size)])
        step *= 2
    return total


def _frozen_term(cotangent, weight, axis, size, ready=None):
    if size & (size - 1) != 0:
        partial = lax.dot_general(
            cotangent, weight, (((1,), (1,)), ((), ())), preferred_element_type=jnp.float32
        )
        return lax.psum_scatter(partial, axis, scatter_dimension=1, tiled=True), ready
    me = lax.axis_index(axis)
    rows = weight.shape[0] // size

    def term(block):
        piece = lax.dynamic_slice_in_dim(weight, block * rows, rows, axis=0)
        return lax.dot_general(
            cotangent, piece, (((1,), (1,)), ((), ())), preferred_element_type=jnp.float32
        )

    held = [term(me ^ e) for e in range(size)]
    step = 0
    while len(held) > 1:
        if step == 1 and ready is not None:
            *leaving, ready = lax.optimization_barrier((*held[1::2], ready))
            held[1::2] = leaving
        partner = 1 << step
        pairs = [(i, i ^ partner) for i in range(size)]
        got = [lax.ppermute(held[e], axis, pairs) for e in range(1, len(held), 2)]
        held = [held[e] + g for e, g in zip(range(0, len(held), 2), got)]
        step += 1
    return held[0], ready


def on_device(
    inputs, cotangent, frozen_key_weight, adapter_down_weight, adapter_up_weight, tenant_per_block
):
    token_row_count, width_portion = inputs.shape
    key_portion = cotangent.shape[1]
    block_count = tenant_per_block.shape[0]
    block_rows = token_row_count // block_count
    adapter_rank_size = adapter_down_weight.shape[1]
    held_tenants = adapter_down_weight.shape[0]
    dp_size = lax.axis_size("dp")
    tensor_size = lax.axis_size("tensor")
    tenant_number = dp_size * held_tenants
    me_dp = lax.axis_index("dp")


    packed = jnp.concatenate([adapter_down_weight, adapter_up_weight], axis=2)
    mirror = block_count == 1 and dp_size >= 4 and dp_size & (dp_size - 1) == 0
    if mirror:
        return _mirrored(
            inputs, cotangent, frozen_key_weight, packed, tenant_per_block,
            width_portion, adapter_rank_size, held_tenants, dp_size, tensor_size,
        )
    stacked, order = _gather_dp(packed, "dp", dp_size)
    stacked = stacked.reshape(dp_size, held_tenants, *packed.shape[1:])
    owner = tenant_per_block // held_tenants
    local = tenant_per_block % held_tenants
    pick = (order[None, :] == owner[:, None])
    pick = pick[:, :, None] & (jnp.arange(held_tenants)[None, None, :] == local[:, None, None])
    pick = pick.reshape(block_count, dp_size * held_tenants).astype(jnp.bfloat16)
    flat = stacked.reshape(dp_size * held_tenants, adapter_rank_size, width_portion + key_portion)
    selected = jnp.einsum("bk,krd->brd", pick, flat, preferred_element_type=jnp.float32).astype(jnp.bfloat16)
    sel_down = selected[:, :, :width_portion]
    sel_up = selected[:, :, width_portion:]

    input_blocks = inputs.reshape(block_count, block_rows, width_portion)
    cotangent_blocks = cotangent.reshape(block_count, block_rows, key_portion)
    low_in = jnp.einsum("bnd,brd->bnr", input_blocks, sel_down, preferred_element_type=jnp.float32)
    reduced_output = ADAPTER_SCALE * jnp.einsum(
        "bnk,brk->bnr", cotangent_blocks, sel_up, preferred_element_type=jnp.float32
    )
    lows = jnp.concatenate([low_in, reduced_output], axis=2)
    base_grad, lows = _frozen_term(cotangent, frozen_key_weight, "tensor", tensor_size, lows)
    lows = _psum_small(lows, "tensor", tensor_size)
    reduced_input_batch = lows[:, :, :adapter_rank_size].astype(jnp.bfloat16)
    low_out_b = lows[:, :, adapter_rank_size:].astype(jnp.bfloat16)

    adapter_grad = jnp.einsum(
        "bnr,brd->bnd", low_out_b, sel_down, preferred_element_type=jnp.float32
    )
    adapter_grad = adapter_grad.reshape(token_row_count, width_portion)
    grad_inputs = (base_grad + adapter_grad).astype(jnp.bfloat16)

    all_tenants = jnp.arange(tenant_number, dtype=jnp.int32)
    member = tenant_per_block[:, None] == all_tenants[None, :]
    member_b = member.astype(jnp.bfloat16)
    weighted_out = (member_b[:, None, :, None] * low_out_b[:, :, None, :]).reshape(
        token_row_count, tenant_number * adapter_rank_size
    )
    weighted_in = (member_b[:, None, :, None] * reduced_input_batch[:, :, None, :]).reshape(
        token_row_count, tenant_number * adapter_rank_size
    )
    down_contribution = lax.dot_general(
        weighted_out, inputs, (((0,), (0,)), ((), ())), preferred_element_type=jnp.float32
    )
    up_contribution = ADAPTER_SCALE * lax.dot_general(
        weighted_in, cotangent, (((0,), (0,)), ((), ())), preferred_element_type=jnp.float32
    )
    down_contribution = down_contribution.reshape(dp_size, held_tenants, adapter_rank_size, width_portion)
    up_contribution = up_contribution.reshape(dp_size, held_tenants, adapter_rank_size, key_portion)
    combined = jnp.concatenate([down_contribution, up_contribution], axis=3)
    owned = lax.dynamic_index_in_dim(combined, me_dp, 0, keepdims=False)
    grad_down = owned[:, :, :width_portion]
    grad_up = owned[:, :, width_portion:]
    for shift, pairs in _partners(dp_size):
        outgoing = lax.dynamic_index_in_dim(combined, _dest_of(me_dp, shift, dp_size), 0, keepdims=False)
        arrived = lax.ppermute(outgoing.astype(jnp.bfloat16), "dp", pairs).astype(jnp.float32)
        grad_down = grad_down + arrived[:, :, :width_portion]
        grad_up = grad_up + arrived[:, :, width_portion:]
    return (grad_inputs, grad_down, grad_up)


def _low_rank(inputs, cotangent, frozen_key_weight, sel_down, sel_up, tensor_size):
    low_in = jnp.dot(inputs, sel_down.T, preferred_element_type=jnp.float32)
    reduced_output = ADAPTER_SCALE * jnp.dot(cotangent, sel_up.T, preferred_element_type=jnp.float32)
    lows = jnp.concatenate([low_in, reduced_output], axis=1)
    base_grad, lows = _frozen_term(cotangent, frozen_key_weight, "tensor", tensor_size, lows)
    lows = _psum_small(lows, "tensor", tensor_size)
    rank = sel_down.shape[0]
    low_in_b = lows[:, :rank].astype(jnp.bfloat16)
    low_out_b = lows[:, rank:].astype(jnp.bfloat16)
    adapter_grad = jnp.dot(low_out_b, sel_down, preferred_element_type=jnp.float32)
    grad_inputs = (base_grad + adapter_grad).astype(jnp.bfloat16)
    return grad_inputs, low_in_b, low_out_b


def _mirrored(
    inputs, cotangent, frozen_key_weight, packed, tenant_per_block,
    width_portion, rank, held_tenants, dp_size, tensor_size,
):
    half = dp_size // 2
    me = lax.axis_index("dp")
    tenant = tenant_per_block[0]
    owner = tenant // held_tenants
    local = tenant % held_tenants
    digits = jnp.zeros((held_tenants, rank, 128), jnp.float32)
    digits = digits.at[:, 0, 0].set((tenant // 256).astype(jnp.float32))
    digits = digits.at[:, 0, 1].set((tenant % 256).astype(jnp.float32))
    payload = jnp.concatenate([packed, digits.astype(packed.dtype)], axis=2)
    mirror_tenant = lax.ppermute(tenant_per_block, "dp", [(i, i ^ half) for i in range(dp_size)])[0]
    within = [payload] + [
        lax.ppermute(payload, "dp", [(i, i ^ s) for i in range(dp_size)]) for s in range(1, half)
    ]
    width = packed.shape[2]
    tenants_within = [
        (w[0, 0, width].astype(jnp.int32) * 256 + w[0, 0, width + 1].astype(jnp.int32))
        for w in within
    ]
    adapters_within = jnp.stack([w[:, :, :width] for w in within], 0)

    def pick(tenant_id):
        slot = (tenant_id // held_tenants) ^ me
        entry = lax.dynamic_index_in_dim(adapters_within, jnp.clip(slot, 0, half - 1), 0, keepdims=False)
        return lax.dynamic_index_in_dim(entry, tenant_id % held_tenants, 0, keepdims=False)

    crossed = lax.ppermute(pick(mirror_tenant), "dp", [(i, i ^ half) for i in range(dp_size)])
    near = ((owner ^ me) < half)
    selected = jnp.where(near, pick(tenant), crossed)
    sel_down = selected[:, :width_portion]
    sel_up = selected[:, width_portion:]

    grad_inputs, low_in_b, low_out_b = _low_rank(
        inputs, cotangent, frozen_key_weight, sel_down, sel_up, tensor_size
    )

    down_term = jnp.dot(low_out_b.T, inputs, preferred_element_type=jnp.float32)
    up_term = ADAPTER_SCALE * jnp.dot(low_in_b.T, cotangent, preferred_element_type=jnp.float32)
    term = jnp.concatenate([down_term, up_term], axis=1)
    slots = jnp.arange(held_tenants)[:, None, None] == local
    term = jnp.where(slots, term[None], 0.0)
    zero = jnp.zeros_like(term)
    own_sum = jnp.where(owner == me, term, zero)
    cross_sum = jnp.where(owner == (me ^ half), term, zero)
    for s in range(1, half):
        mate = me ^ s
        outgoing = jnp.where((owner == mate) | (owner == (mate ^ half)), term, zero)
        arrived = lax.ppermute(outgoing, "dp", [(i, i ^ s) for i in range(dp_size)])
        sender_owner = tenants_within[s] // held_tenants
        own_sum = own_sum + jnp.where(sender_owner == me, arrived, zero)
        cross_sum = cross_sum + jnp.where(sender_owner == (me ^ half), arrived, zero)
    arrived = lax.ppermute(cross_sum.astype(jnp.bfloat16), "dp", [(i, i ^ half) for i in range(dp_size)])
    grad_down = own_sum[:, :, :width_portion] + arrived[:, :, :width_portion].astype(jnp.float32)
    grad_up = own_sum[:, :, width_portion:] + arrived[:, :, width_portion:].astype(jnp.float32)
    inputs_shape = inputs.shape
    return (grad_inputs.reshape(inputs_shape), grad_down, grad_up)


def solution(mesh):
    in_specs = (
        P("dp", "tensor"),
        P("dp", "tensor"),
        P(None, "tensor"),
        P("dp", None, "tensor"),
        P("dp", None, "tensor"),
        P("dp"),
    )
    out_specs = (P("dp", "tensor"), P("dp", None, "tensor"), P("dp", None, "tensor"))
    return jax.shard_map(
        on_device, mesh=mesh, in_specs=in_specs, out_specs=out_specs, check_vma=False
    )
```

```python
import jax
import jax.numpy as jnp
from jax import lax
from jax.sharding import PartitionSpec as P

ADAPTER_SCALE = 2.0


def _partners(size):
    if size & (size - 1) == 0:
        return [(s, [(i, i ^ s) for i in range(size)]) for s in range(1, size)]
    return [(s, [(i, (i + s) % size) for i in range(size)]) for s in range(1, size)]


def _source_of(me, shift, size):
    if size & (size - 1) == 0:
        return me ^ shift
    return (me - shift + size) % size


def _dest_of(me, shift, size):
    if size & (size - 1) == 0:
        return me ^ shift
    return (me + shift) % size


def _gather_dp(local, axis, size):
    me = lax.axis_index(axis)
    if size & (size - 1) != 0 or size < 4:
        got = [local]
        sources = [me]
        for shift, pairs in _partners(size):
            got.append(lax.ppermute(local, axis, pairs))
            sources.append(_source_of(me, shift, size))
        return jnp.stack(got, 0), jnp.stack(sources)
    pair = jnp.concatenate([local, lax.ppermute(local, axis, [(i, i ^ 1) for i in range(size)])], 0)
    got = [pair]
    sources = [me, me ^ 1]
    for m in range(1, size // 2):
        shift = 2 * m
        got.append(lax.ppermute(pair, axis, [(i, i ^ shift) for i in range(size)]))
        sources += [me ^ shift, me ^ shift ^ 1]
    return jnp.concatenate(got, 0), jnp.stack(sources)


def _psum_small(value, axis, size):
    if size & (size - 1) != 0:
        total = value
        for _, pairs in _partners(size):
            total = total + lax.ppermute(value, axis, pairs)
        return total
    total = value
    step = 1
    while step < size:
        total = total + lax.ppermute(total, axis, [(i, i ^ step) for i in range(size)])
        step *= 2
    return total


def _frozen_term(cotangent, weight, axis, size, ready=None):
    if size & (size - 1) != 0:
        partial = lax.dot_general(
            cotangent, weight, (((1,), (1,)), ((), ())), preferred_element_type=jnp.float32
        )
        return lax.psum_scatter(partial, axis, scatter_dimension=1, tiled=True), ready
    me = lax.axis_index(axis)
    rows = weight.shape[0] // size

    def term(block):
        piece = lax.dynamic_slice_in_dim(weight, block * rows, rows, axis=0)
        return lax.dot_general(
            cotangent, piece, (((1,), (1,)), ((), ())), preferred_element_type=jnp.float32
        )

    held = [term(me ^ e) for e in range(size)]
    step = 0
    while len(held) > 1:
        if step == 1 and ready is not None:
            *leaving, ready = lax.optimization_barrier((*held[1::2], ready))
            held[1::2] = leaving
        partner = 1 << step
        pairs = [(i, i ^ partner) for i in range(size)]
        got = [lax.ppermute(held[e], axis, pairs) for e in range(1, len(held), 2)]
        held = [held[e] + g for e, g in zip(range(0, len(held), 2), got)]
        step += 1
    return held[0], ready


def on_device(
    inputs, cotangent, frozen_key_weight, adapter_down_weight, adapter_up_weight, tenant_per_block
):
    token_row_count, width_portion = inputs.shape
    key_portion = cotangent.shape[1]
    block_count = tenant_per_block.shape[0]
    block_rows = token_row_count // block_count
    adapter_rank_size = adapter_down_weight.shape[1]
    held_tenants = adapter_down_weight.shape[0]
    dp_size = lax.axis_size("dp")
    tensor_size = lax.axis_size("tensor")
    tenant_number = dp_size * held_tenants
    me_dp = lax.axis_index("dp")


    packed = jnp.concatenate([adapter_down_weight, adapter_up_weight], axis=2)
    mirror = block_count == 1 and dp_size >= 4 and dp_size & (dp_size - 1) == 0
    if mirror:
        return _mirrored(
            inputs, cotangent, frozen_key_weight, packed, tenant_per_block,
            width_portion, adapter_rank_size, held_tenants, dp_size, tensor_size,
        )
    stacked, order = _gather_dp(packed, "dp", dp_size)
    stacked = stacked.reshape(dp_size, held_tenants, *packed.shape[1:])
    owner = tenant_per_block // held_tenants
    local = tenant_per_block % held_tenants
    pick = (order[None, :] == owner[:, None])
    pick = pick[:, :, None] & (jnp.arange(held_tenants)[None, None, :] == local[:, None, None])
    pick = pick.reshape(block_count, dp_size * held_tenants).astype(jnp.bfloat16)
    flat = stacked.reshape(dp_size * held_tenants, adapter_rank_size, width_portion + key_portion)
    selected = jnp.einsum("bk,krd->brd", pick, flat, preferred_element_type=jnp.float32).astype(jnp.bfloat16)
    sel_down = selected[:, :, :width_portion]
    sel_up = selected[:, :, width_portion:]

    input_blocks = inputs.reshape(block_count, block_rows, width_portion)
    cotangent_blocks = cotangent.reshape(block_count, block_rows, key_portion)
    low_in = jnp.einsum("bnd,brd->bnr", input_blocks, sel_down, preferred_element_type=jnp.float32)
    reduced_output = ADAPTER_SCALE * jnp.einsum(
        "bnk,brk->bnr", cotangent_blocks, sel_up, preferred_element_type=jnp.float32
    )
    lows = jnp.concatenate([low_in, reduced_output], axis=2)
    base_grad, lows = _frozen_term(cotangent, frozen_key_weight, "tensor", tensor_size, lows)
    lows = _psum_small(lows, "tensor", tensor_size)
    reduced_input_batch = lows[:, :, :adapter_rank_size].astype(jnp.bfloat16)
    low_out_b = lows[:, :, adapter_rank_size:].astype(jnp.bfloat16)

    adapter_grad = jnp.einsum(
        "bnr,brd->bnd", low_out_b, sel_down, preferred_element_type=jnp.float32
    )
    adapter_grad = adapter_grad.reshape(token_row_count, width_portion)
    grad_inputs = (base_grad + adapter_grad).astype(jnp.bfloat16)

    all_tenants = jnp.arange(tenant_number, dtype=jnp.int32)
    member = tenant_per_block[:, None] == all_tenants[None, :]
    member_b = member.astype(jnp.bfloat16)
    weighted_out = (member_b[:, None, :, None] * low_out_b[:, :, None, :]).reshape(
        token_row_count, tenant_number * adapter_rank_size
    )
    weighted_in = (member_b[:, None, :, None] * reduced_input_batch[:, :, None, :]).reshape(
        token_row_count, tenant_number * adapter_rank_size
    )
    down_contribution = lax.dot_general(
        weighted_out, inputs, (((0,), (0,)), ((), ())), preferred_element_type=jnp.float32
    )
    up_contribution = ADAPTER_SCALE * lax.dot_general(
        weighted_in, cotangent, (((0,), (0,)), ((), ())), preferred_element_type=jnp.float32
    )
    down_contribution = down_contribution.reshape(dp_size, held_tenants, adapter_rank_size, width_portion)
    up_contribution = up_contribution.reshape(dp_size, held_tenants, adapter_rank_size, key_portion)
    combined = jnp.concatenate([down_contribution, up_contribution], axis=3)
    owned = lax.dynamic_index_in_dim(combined, me_dp, 0, keepdims=False)
    grad_down = owned[:, :, :width_portion]
    grad_up = owned[:, :, width_portion:]
    for shift, pairs in _partners(dp_size):
        outgoing = lax.dynamic_index_in_dim(combined, _dest_of(me_dp, shift, dp_size), 0, keepdims=False)
        arrived = lax.ppermute(outgoing.astype(jnp.bfloat16), "dp", pairs).astype(jnp.float32)
        grad_down = grad_down + arrived[:, :, :width_portion]
        grad_up = grad_up + arrived[:, :, width_portion:]
    return (grad_inputs, grad_down, grad_up)


def _frozen_first(cotangent, weight, axis, size):
    me = lax.axis_index(axis)
    rows = weight.shape[0] // size

    def term(block):
        piece = lax.dynamic_slice_in_dim(weight, block * rows, rows, axis=0)
        return lax.dot_general(
            cotangent, piece, (((1,), (1,)), ((), ())), preferred_element_type=jnp.float32
        )

    pieces = [lax.dynamic_slice_in_dim(weight, (me ^ e) * rows, rows, axis=0) for e in range(1, size, 2)]
    leaving = jnp.einsum(
        "nk,bdk->bnd", cotangent, jnp.stack(pieces, 0), preferred_element_type=jnp.float32
    )
    got = lax.ppermute(leaving, axis, [(i, i ^ 1) for i in range(size)])
    return [term(me ^ e) + got[m] for m, e in enumerate(range(0, size, 2))]


def _frozen_rest(held, axis, size):
    step = 1
    while len(held) > 1:
        partner = 1 << step
        pairs = [(i, i ^ partner) for i in range(size)]
        got = [lax.ppermute(held[e], axis, pairs) for e in range(1, len(held), 2)]
        held = [held[e] + g for e, g in zip(range(0, len(held), 2), got)]
        step += 1
    return held[0]


def _low_rank(inputs, cotangent, base_grad, sel_down, sel_up, tensor_size):
    low_in = jnp.dot(inputs, sel_down.T, preferred_element_type=jnp.float32)
    reduced_output = ADAPTER_SCALE * jnp.dot(cotangent, sel_up.T, preferred_element_type=jnp.float32)
    lows = jnp.concatenate([low_in, reduced_output], axis=1)
    lows = _psum_small(lows, "tensor", tensor_size)
    rank = sel_down.shape[0]
    low_in_b = lows[:, :rank].astype(jnp.bfloat16)
    low_out_b = lows[:, rank:].astype(jnp.bfloat16)
    adapter_grad = jnp.dot(low_out_b, sel_down, preferred_element_type=jnp.float32)
    grad_inputs = (base_grad + adapter_grad).astype(jnp.bfloat16)
    return grad_inputs, low_in_b, low_out_b


def _mirrored(
    inputs, cotangent, frozen_key_weight, packed, tenant_per_block,
    width_portion, rank, held_tenants, dp_size, tensor_size,
):
    half = dp_size // 2
    me = lax.axis_index("dp")
    tenant = tenant_per_block[0]
    owner = tenant // held_tenants
    local = tenant % held_tenants
    digits = jnp.zeros((held_tenants, rank, 128), jnp.float32)
    digits = digits.at[:, 0, 0].set((tenant // 256).astype(jnp.float32))
    digits = digits.at[:, 0, 1].set((tenant % 256).astype(jnp.float32))
    payload = jnp.concatenate([packed, digits.astype(packed.dtype)], axis=2)
    mirror_tenant = lax.ppermute(tenant_per_block, "dp", [(i, i ^ half) for i in range(dp_size)])[0]
    within = [payload] + [
        lax.ppermute(payload, "dp", [(i, i ^ s) for i in range(dp_size)]) for s in range(1, half)
    ]
    width = packed.shape[2]
    tenants_within = [
        (w[0, 0, width].astype(jnp.int32) * 256 + w[0, 0, width + 1].astype(jnp.int32))
        for w in within
    ]
    adapters_within = jnp.stack([w[:, :, :width] for w in within], 0)

    def pick(tenant_id):
        slot = (tenant_id // held_tenants) ^ me
        entry = lax.dynamic_index_in_dim(adapters_within, jnp.clip(slot, 0, half - 1), 0, keepdims=False)
        return lax.dynamic_index_in_dim(entry, tenant_id % held_tenants, 0, keepdims=False)

    for_mirror = pick(mirror_tenant)
    halving = tensor_size > 1 and tensor_size & (tensor_size - 1) == 0
    if halving:
        frozen = _frozen_first(cotangent, frozen_key_weight, "tensor", tensor_size)
        *leaving, for_mirror = lax.optimization_barrier((*frozen[1::2], for_mirror))
        frozen[1::2] = leaving
        base_grad = _frozen_rest(frozen, "tensor", tensor_size)
    else:
        partial = lax.dot_general(
            cotangent, frozen_key_weight, (((1,), (1,)), ((), ())), preferred_element_type=jnp.float32
        )
        base_grad = lax.psum_scatter(partial, "tensor", scatter_dimension=1, tiled=True)
    crossed = lax.ppermute(for_mirror, "dp", [(i, i ^ half) for i in range(dp_size)])
    near = ((owner ^ me) < half)
    selected = jnp.where(near, pick(tenant), crossed)
    sel_down = selected[:, :width_portion]
    sel_up = selected[:, width_portion:]

    grad_inputs, low_in_b, low_out_b = _low_rank(
        inputs, cotangent, base_grad, sel_down, sel_up, tensor_size
    )

    down_term = jnp.dot(low_out_b.T, inputs, preferred_element_type=jnp.float32)
    up_term = ADAPTER_SCALE * jnp.dot(low_in_b.T, cotangent, preferred_element_type=jnp.float32)
    term = jnp.concatenate([down_term, up_term], axis=1)
    slots = jnp.arange(held_tenants)[:, None, None] == local
    term = jnp.where(slots, term[None], 0.0)
    zero = jnp.zeros_like(term)
    own_sum = jnp.where(owner == me, term, zero)
    cross_sum = jnp.where(owner == (me ^ half), term, zero)
    for s in range(1, half):
        mate = me ^ s
        outgoing = jnp.where((owner == mate) | (owner == (mate ^ half)), term, zero)
        arrived = lax.ppermute(outgoing, "dp", [(i, i ^ s) for i in range(dp_size)])
        sender_owner = tenants_within[s] // held_tenants
        own_sum = own_sum + jnp.where(sender_owner == me, arrived, zero)
        cross_sum = cross_sum + jnp.where(sender_owner == (me ^ half), arrived, zero)
    arrived = lax.ppermute(cross_sum.astype(jnp.bfloat16), "dp", [(i, i ^ half) for i in range(dp_size)])
    grad_down = own_sum[:, :, :width_portion] + arrived[:, :, :width_portion].astype(jnp.float32)
    grad_up = own_sum[:, :, width_portion:] + arrived[:, :, width_portion:].astype(jnp.float32)
    inputs_shape = inputs.shape
    return (grad_inputs.reshape(inputs_shape), grad_down, grad_up)


def solution(mesh):
    in_specs = (
        P("dp", "tensor"),
        P("dp", "tensor"),
        P(None, "tensor"),
        P("dp", None, "tensor"),
        P("dp", None, "tensor"),
        P("dp"),
    )
    out_specs = (P("dp", "tensor"), P("dp", None, "tensor"), P("dp", None, "tensor"))
    return jax.shard_map(
        on_device, mesh=mesh, in_specs=in_specs, out_specs=out_specs, check_vma=False
    )
```

```python
import jax
import jax.numpy as jnp
from jax import lax
from jax.sharding import PartitionSpec as P

ADAPTER_SCALE = 2.0


def _partners(size):
    if size & (size - 1) == 0:
        return [(s, [(i, i ^ s) for i in range(size)]) for s in range(1, size)]
    return [(s, [(i, (i + s) % size) for i in range(size)]) for s in range(1, size)]


def _source_of(me, shift, size):
    if size & (size - 1) == 0:
        return me ^ shift
    return (me - shift + size) % size


def _dest_of(me, shift, size):
    if size & (size - 1) == 0:
        return me ^ shift
    return (me + shift) % size


def _gather_dp(local, axis, size):
    me = lax.axis_index(axis)
    if size & (size - 1) != 0 or size < 4:
        got = [local]
        sources = [me]
        for shift, pairs in _partners(size):
            got.append(lax.ppermute(local, axis, pairs))
            sources.append(_source_of(me, shift, size))
        return jnp.stack(got, 0), jnp.stack(sources)
    pair = jnp.concatenate([local, lax.ppermute(local, axis, [(i, i ^ 1) for i in range(size)])], 0)
    got = [pair]
    sources = [me, me ^ 1]
    for m in range(1, size // 2):
        shift = 2 * m
        got.append(lax.ppermute(pair, axis, [(i, i ^ shift) for i in range(size)]))
        sources += [me ^ shift, me ^ shift ^ 1]
    return jnp.concatenate(got, 0), jnp.stack(sources)


def _psum_small(value, axis, size):
    if size & (size - 1) != 0:
        total = value
        for _, pairs in _partners(size):
            total = total + lax.ppermute(value, axis, pairs)
        return total
    total = value
    step = 1
    while step < size:
        total = total + lax.ppermute(total, axis, [(i, i ^ step) for i in range(size)])
        step *= 2
    return total


def _frozen_term(cotangent, weight, axis, size, ready=None):
    if size & (size - 1) != 0:
        partial = lax.dot_general(
            cotangent, weight, (((1,), (1,)), ((), ())), preferred_element_type=jnp.float32
        )
        return lax.psum_scatter(partial, axis, scatter_dimension=1, tiled=True), ready
    me = lax.axis_index(axis)
    rows = weight.shape[0] // size

    def term(block):
        piece = lax.dynamic_slice_in_dim(weight, block * rows, rows, axis=0)
        return lax.dot_general(
            cotangent, piece, (((1,), (1,)), ((), ())), preferred_element_type=jnp.float32
        )

    held = [term(me ^ e) for e in range(size)]
    step = 0
    while len(held) > 1:
        if step == 1 and ready is not None:
            *leaving, ready = lax.optimization_barrier((*held[1::2], ready))
            held[1::2] = leaving
        partner = 1 << step
        pairs = [(i, i ^ partner) for i in range(size)]
        got = [lax.ppermute(held[e], axis, pairs) for e in range(1, len(held), 2)]
        held = [held[e] + g for e, g in zip(range(0, len(held), 2), got)]
        step += 1
    return held[0], ready


def on_device(
    inputs, cotangent, frozen_key_weight, adapter_down_weight, adapter_up_weight, tenant_per_block
):
    token_row_count, width_portion = inputs.shape
    key_portion = cotangent.shape[1]
    block_count = tenant_per_block.shape[0]
    block_rows = token_row_count // block_count
    adapter_rank_size = adapter_down_weight.shape[1]
    held_tenants = adapter_down_weight.shape[0]
    dp_size = lax.axis_size("dp")
    tensor_size = lax.axis_size("tensor")
    tenant_number = dp_size * held_tenants
    me_dp = lax.axis_index("dp")


    packed = jnp.concatenate([adapter_down_weight, adapter_up_weight], axis=2)
    mirror = block_count == 1 and dp_size >= 4 and dp_size & (dp_size - 1) == 0
    if mirror:
        return _mirrored(
            inputs, cotangent, frozen_key_weight, packed, tenant_per_block,
            width_portion, adapter_rank_size, held_tenants, dp_size, tensor_size,
        )
    stacked, order = _gather_dp(packed, "dp", dp_size)
    stacked = stacked.reshape(dp_size, held_tenants, *packed.shape[1:])
    owner = tenant_per_block // held_tenants
    local = tenant_per_block % held_tenants
    pick = (order[None, :] == owner[:, None])
    pick = pick[:, :, None] & (jnp.arange(held_tenants)[None, None, :] == local[:, None, None])
    pick = pick.reshape(block_count, dp_size * held_tenants).astype(jnp.bfloat16)
    flat = stacked.reshape(dp_size * held_tenants, adapter_rank_size, width_portion + key_portion)
    selected = jnp.einsum("bk,krd->brd", pick, flat, preferred_element_type=jnp.float32).astype(jnp.bfloat16)
    sel_down = selected[:, :, :width_portion]
    sel_up = selected[:, :, width_portion:]

    input_blocks = inputs.reshape(block_count, block_rows, width_portion)
    cotangent_blocks = cotangent.reshape(block_count, block_rows, key_portion)
    low_in = jnp.einsum("bnd,brd->bnr", input_blocks, sel_down, preferred_element_type=jnp.float32)
    reduced_output = ADAPTER_SCALE * jnp.einsum(
        "bnk,brk->bnr", cotangent_blocks, sel_up, preferred_element_type=jnp.float32
    )
    lows = jnp.concatenate([low_in, reduced_output], axis=2)
    base_grad, lows = _frozen_term(cotangent, frozen_key_weight, "tensor", tensor_size, lows)
    lows = _psum_small(lows, "tensor", tensor_size)
    reduced_input_batch = lows[:, :, :adapter_rank_size].astype(jnp.bfloat16)
    low_out_b = lows[:, :, adapter_rank_size:].astype(jnp.bfloat16)

    adapter_grad = jnp.einsum(
        "bnr,brd->bnd", low_out_b, sel_down, preferred_element_type=jnp.float32
    )
    adapter_grad = adapter_grad.reshape(token_row_count, width_portion)
    grad_inputs = (base_grad + adapter_grad).astype(jnp.bfloat16)

    all_tenants = jnp.arange(tenant_number, dtype=jnp.int32)
    member = tenant_per_block[:, None] == all_tenants[None, :]
    member_b = member.astype(jnp.bfloat16)
    weighted_out = (member_b[:, None, :, None] * low_out_b[:, :, None, :]).reshape(
        token_row_count, tenant_number * adapter_rank_size
    )
    weighted_in = (member_b[:, None, :, None] * reduced_input_batch[:, :, None, :]).reshape(
        token_row_count, tenant_number * adapter_rank_size
    )
    down_contribution = lax.dot_general(
        weighted_out, inputs, (((0,), (0,)), ((), ())), preferred_element_type=jnp.float32
    )
    up_contribution = ADAPTER_SCALE * lax.dot_general(
        weighted_in, cotangent, (((0,), (0,)), ((), ())), preferred_element_type=jnp.float32
    )
    down_contribution = down_contribution.reshape(dp_size, held_tenants, adapter_rank_size, width_portion)
    up_contribution = up_contribution.reshape(dp_size, held_tenants, adapter_rank_size, key_portion)
    combined = jnp.concatenate([down_contribution, up_contribution], axis=3)
    owned = lax.dynamic_index_in_dim(combined, me_dp, 0, keepdims=False)
    grad_down = owned[:, :, :width_portion]
    grad_up = owned[:, :, width_portion:]
    for shift, pairs in _partners(dp_size):
        outgoing = lax.dynamic_index_in_dim(combined, _dest_of(me_dp, shift, dp_size), 0, keepdims=False)
        arrived = lax.ppermute(outgoing.astype(jnp.bfloat16), "dp", pairs).astype(jnp.float32)
        grad_down = grad_down + arrived[:, :, :width_portion]
        grad_up = grad_up + arrived[:, :, width_portion:]
    return (grad_inputs, grad_down, grad_up)


def _frozen_first(cotangent, weight, axis, size):
    me = lax.axis_index(axis)
    rows = weight.shape[0] // size

    def term(block):
        piece = lax.dynamic_slice_in_dim(weight, block * rows, rows, axis=0)
        return lax.dot_general(
            cotangent, piece, (((1,), (1,)), ((), ())), preferred_element_type=jnp.float32
        )

    pieces = [lax.dynamic_slice_in_dim(weight, (me ^ e) * rows, rows, axis=0) for e in range(1, size, 2)]
    leaving = jnp.einsum(
        "nk,bdk->bnd", cotangent, jnp.stack(pieces, 0), preferred_element_type=jnp.float32
    )
    got = lax.ppermute(leaving, axis, [(i, i ^ 1) for i in range(size)])
    return [term(me ^ e) + got[m] for m, e in enumerate(range(0, size, 2))]


def _frozen_rest(held, axis, size):
    step = 1
    while len(held) > 1:
        partner = 1 << step
        pairs = [(i, i ^ partner) for i in range(size)]
        got = [lax.ppermute(held[e], axis, pairs) for e in range(1, len(held), 2)]
        held = [held[e] + g for e, g in zip(range(0, len(held), 2), got)]
        step += 1
    return held[0]


def _low_rank(inputs, cotangent, frozen_key_weight, sel_down, sel_up, tensor_size):
    low_in = jnp.dot(inputs, sel_down.T, preferred_element_type=jnp.float32)
    reduced_output = ADAPTER_SCALE * jnp.dot(cotangent, sel_up.T, preferred_element_type=jnp.float32)
    lows = jnp.concatenate([low_in, reduced_output], axis=1)
    if tensor_size > 1 and tensor_size & (tensor_size - 1) == 0:
        frozen = _frozen_first(cotangent, frozen_key_weight, "tensor", tensor_size)
        *leaving, lows = lax.optimization_barrier((*frozen[1::2], lows))
        frozen[1::2] = leaving
        base_grad = _frozen_rest(frozen, "tensor", tensor_size)
    else:
        partial = lax.dot_general(
            cotangent, frozen_key_weight, (((1,), (1,)), ((), ())), preferred_element_type=jnp.float32
        )
        base_grad = lax.psum_scatter(partial, "tensor", scatter_dimension=1, tiled=True)
    lows = _psum_small(lows, "tensor", tensor_size)
    rank = sel_down.shape[0]
    low_in_b = lows[:, :rank].astype(jnp.bfloat16)
    low_out_b = lows[:, rank:].astype(jnp.bfloat16)
    adapter_grad = jnp.dot(low_out_b, sel_down, preferred_element_type=jnp.float32)
    grad_inputs = (base_grad + adapter_grad).astype(jnp.bfloat16)
    return grad_inputs, low_in_b, low_out_b


def _mirrored(
    inputs, cotangent, frozen_key_weight, packed, tenant_per_block,
    width_portion, rank, held_tenants, dp_size, tensor_size,
):
    half = dp_size // 2
    me = lax.axis_index("dp")
    tenant = tenant_per_block[0]
    owner = tenant // held_tenants
    local = tenant % held_tenants
    digits = jnp.zeros((held_tenants, rank, 128), jnp.float32)
    digits = digits.at[:, 0, 0].set((tenant // 256).astype(jnp.float32))
    digits = digits.at[:, 0, 1].set((tenant % 256).astype(jnp.float32))
    payload = jnp.concatenate([packed, digits.astype(packed.dtype)], axis=2)
    mirror_tenant = lax.ppermute(tenant_per_block, "dp", [(i, i ^ half) for i in range(dp_size)])[0]
    within = [payload] + [
        lax.ppermute(payload, "dp", [(i, i ^ s) for i in range(dp_size)]) for s in range(1, half)
    ]
    width = packed.shape[2]
    tenants_within = [
        (w[0, 0, width].astype(jnp.int32) * 256 + w[0, 0, width + 1].astype(jnp.int32))
        for w in within
    ]
    adapters_within = jnp.stack([w[:, :, :width] for w in within], 0)

    def pick(tenant_id):
        slot = (tenant_id // held_tenants) ^ me
        entry = lax.dynamic_index_in_dim(adapters_within, jnp.clip(slot, 0, half - 1), 0, keepdims=False)
        return lax.dynamic_index_in_dim(entry, tenant_id % held_tenants, 0, keepdims=False)

    crossed = lax.ppermute(pick(mirror_tenant), "dp", [(i, i ^ half) for i in range(dp_size)])
    near = ((owner ^ me) < half)
    selected = jnp.where(near, pick(tenant), crossed)
    sel_down = selected[:, :width_portion]
    sel_up = selected[:, width_portion:]

    grad_inputs, low_in_b, low_out_b = _low_rank(
        inputs, cotangent, frozen_key_weight, sel_down, sel_up, tensor_size
    )

    down_term = jnp.dot(low_out_b.T, inputs, preferred_element_type=jnp.float32)
    up_term = ADAPTER_SCALE * jnp.dot(low_in_b.T, cotangent, preferred_element_type=jnp.float32)
    term = jnp.concatenate([down_term, up_term], axis=1)
    slots = jnp.arange(held_tenants)[:, None, None] == local
    term = jnp.where(slots, term[None], 0.0)
    zero = jnp.zeros_like(term)
    own_sum = jnp.where(owner == me, term, zero)
    cross_sum = jnp.where(owner == (me ^ half), term, zero)
    for s in range(1, half):
        mate = me ^ s
        outgoing = jnp.where((owner == mate) | (owner == (mate ^ half)), term, zero)
        arrived = lax.ppermute(outgoing, "dp", [(i, i ^ s) for i in range(dp_size)])
        sender_owner = tenants_within[s] // held_tenants
        own_sum = own_sum + jnp.where(sender_owner == me, arrived, zero)
        cross_sum = cross_sum + jnp.where(sender_owner == (me ^ half), arrived, zero)
    arrived = lax.ppermute(cross_sum.astype(jnp.bfloat16), "dp", [(i, i ^ half) for i in range(dp_size)])
    grad_down = own_sum[:, :, :width_portion] + arrived[:, :, :width_portion].astype(jnp.float32)
    grad_up = own_sum[:, :, width_portion:] + arrived[:, :, width_portion:].astype(jnp.float32)
    inputs_shape = inputs.shape
    return (grad_inputs.reshape(inputs_shape), grad_down, grad_up)


def solution(mesh):
    in_specs = (
        P("dp", "tensor"),
        P("dp", "tensor"),
        P(None, "tensor"),
        P("dp", None, "tensor"),
        P("dp", None, "tensor"),
        P("dp"),
    )
    out_specs = (P("dp", "tensor"), P("dp", None, "tensor"), P("dp", None, "tensor"))
    return jax.shard_map(
        on_device, mesh=mesh, in_specs=in_specs, out_specs=out_specs, check_vma=False
    )
```

```python
import jax
import jax.numpy as jnp
from jax import lax
from jax.sharding import PartitionSpec as P

ADAPTER_SCALE = 2.0


def _partners(size):
    if size & (size - 1) == 0:
        return [(s, [(i, i ^ s) for i in range(size)]) for s in range(1, size)]
    return [(s, [(i, (i + s) % size) for i in range(size)]) for s in range(1, size)]


def _source_of(me, shift, size):
    if size & (size - 1) == 0:
        return me ^ shift
    return (me - shift + size) % size


def _dest_of(me, shift, size):
    if size & (size - 1) == 0:
        return me ^ shift
    return (me + shift) % size


def _gather_dp(local, axis, size):
    me = lax.axis_index(axis)
    if size & (size - 1) != 0 or size < 4:
        got = [local]
        sources = [me]
        for shift, pairs in _partners(size):
            got.append(lax.ppermute(local, axis, pairs))
            sources.append(_source_of(me, shift, size))
        return jnp.stack(got, 0), jnp.stack(sources)
    pair = jnp.concatenate([local, lax.ppermute(local, axis, [(i, i ^ 1) for i in range(size)])], 0)
    got = [pair]
    sources = [me, me ^ 1]
    for m in range(1, size // 2):
        shift = 2 * m
        got.append(lax.ppermute(pair, axis, [(i, i ^ shift) for i in range(size)]))
        sources += [me ^ shift, me ^ shift ^ 1]
    return jnp.concatenate(got, 0), jnp.stack(sources)


def _psum_small(value, axis, size):
    if size & (size - 1) != 0:
        total = value
        for _, pairs in _partners(size):
            total = total + lax.ppermute(value, axis, pairs)
        return total
    total = value
    step = 1
    while step < size:
        total = total + lax.ppermute(total, axis, [(i, i ^ step) for i in range(size)])
        step *= 2
    return total


def _frozen_term(cotangent, weight, axis, size, ready=None):
    if size & (size - 1) != 0:
        partial = lax.dot_general(
            cotangent, weight, (((1,), (1,)), ((), ())), preferred_element_type=jnp.float32
        )
        return lax.psum_scatter(partial, axis, scatter_dimension=1, tiled=True), ready
    me = lax.axis_index(axis)
    rows = weight.shape[0] // size

    def term(block):
        piece = lax.dynamic_slice_in_dim(weight, block * rows, rows, axis=0)
        return lax.dot_general(
            cotangent, piece, (((1,), (1,)), ((), ())), preferred_element_type=jnp.float32
        )

    held = [term(me ^ e) for e in range(size)]
    step = 0
    while len(held) > 1:
        if step == 1 and ready is not None:
            *leaving, ready = lax.optimization_barrier((*held[1::2], ready))
            held[1::2] = leaving
        partner = 1 << step
        pairs = [(i, i ^ partner) for i in range(size)]
        got = [lax.ppermute(held[e], axis, pairs) for e in range(1, len(held), 2)]
        held = [held[e] + g for e, g in zip(range(0, len(held), 2), got)]
        step += 1
    return held[0], ready


def on_device(
    inputs, cotangent, frozen_key_weight, adapter_down_weight, adapter_up_weight, tenant_per_block
):
    token_row_count, width_portion = inputs.shape
    key_portion = cotangent.shape[1]
    block_count = tenant_per_block.shape[0]
    block_rows = token_row_count // block_count
    adapter_rank_size = adapter_down_weight.shape[1]
    held_tenants = adapter_down_weight.shape[0]
    dp_size = lax.axis_size("dp")
    tensor_size = lax.axis_size("tensor")
    tenant_number = dp_size * held_tenants
    me_dp = lax.axis_index("dp")


    packed = jnp.concatenate([adapter_down_weight, adapter_up_weight], axis=2)
    width = packed.shape[2]
    routed = block_count == 1 and dp_size >= 4 and dp_size & (dp_size - 1) == 0
    if routed:
        tenant = tenant_per_block[0]
        digits = jnp.zeros((held_tenants, adapter_rank_size, 128), jnp.float32)
        digits = digits.at[:, 0, 0].set((tenant // 256).astype(jnp.float32))
        digits = digits.at[:, 0, 1].set((tenant % 256).astype(jnp.float32))
        packed = jnp.concatenate([packed, digits.astype(packed.dtype)], axis=2)
    stacked, order = _gather_dp(packed, "dp", dp_size)
    stacked = stacked.reshape(dp_size, held_tenants, *packed.shape[1:])
    if routed:
        tenants_seen = [
            stacked[p, 0, 0, width].astype(jnp.int32) * 256 + stacked[p, 0, 0, width + 1].astype(jnp.int32)
            for p in range(dp_size)
        ]
        stacked = stacked[..., :width]
    owner = tenant_per_block // held_tenants
    local = tenant_per_block % held_tenants
    pick = (order[None, :] == owner[:, None])
    pick = pick[:, :, None] & (jnp.arange(held_tenants)[None, None, :] == local[:, None, None])
    pick = pick.reshape(block_count, dp_size * held_tenants).astype(jnp.bfloat16)
    flat = stacked.reshape(dp_size * held_tenants, adapter_rank_size, width_portion + key_portion)
    selected = jnp.einsum("bk,krd->brd", pick, flat, preferred_element_type=jnp.float32).astype(jnp.bfloat16)
    sel_down = selected[:, :, :width_portion]
    sel_up = selected[:, :, width_portion:]

    input_blocks = inputs.reshape(block_count, block_rows, width_portion)
    cotangent_blocks = cotangent.reshape(block_count, block_rows, key_portion)
    low_in = jnp.einsum("bnd,brd->bnr", input_blocks, sel_down, preferred_element_type=jnp.float32)
    reduced_output = ADAPTER_SCALE * jnp.einsum(
        "bnk,brk->bnr", cotangent_blocks, sel_up, preferred_element_type=jnp.float32
    )
    lows = jnp.concatenate([low_in, reduced_output], axis=2)
    base_grad, lows = _frozen_term(cotangent, frozen_key_weight, "tensor", tensor_size, lows)
    lows = _psum_small(lows, "tensor", tensor_size)
    reduced_input_batch = lows[:, :, :adapter_rank_size].astype(jnp.bfloat16)
    low_out_b = lows[:, :, adapter_rank_size:].astype(jnp.bfloat16)

    adapter_grad = jnp.einsum(
        "bnr,brd->bnd", low_out_b, sel_down, preferred_element_type=jnp.float32
    )
    adapter_grad = adapter_grad.reshape(token_row_count, width_portion)
    grad_inputs = (base_grad + adapter_grad).astype(jnp.bfloat16)

    all_tenants = jnp.arange(tenant_number, dtype=jnp.int32)
    member = tenant_per_block[:, None] == all_tenants[None, :]
    member_b = member.astype(jnp.bfloat16)
    weighted_out = (member_b[:, None, :, None] * low_out_b[:, :, None, :]).reshape(
        token_row_count, tenant_number * adapter_rank_size
    )
    weighted_in = (member_b[:, None, :, None] * reduced_input_batch[:, :, None, :]).reshape(
        token_row_count, tenant_number * adapter_rank_size
    )
    down_contribution = lax.dot_general(
        weighted_out, inputs, (((0,), (0,)), ((), ())), preferred_element_type=jnp.float32
    )
    up_contribution = ADAPTER_SCALE * lax.dot_general(
        weighted_in, cotangent, (((0,), (0,)), ((), ())), preferred_element_type=jnp.float32
    )
    down_contribution = down_contribution.reshape(dp_size, held_tenants, adapter_rank_size, width_portion)
    up_contribution = up_contribution.reshape(dp_size, held_tenants, adapter_rank_size, key_portion)
    combined = jnp.concatenate([down_contribution, up_contribution], axis=3)
    if routed:
        half = dp_size // 2
        owner_me = tenant_per_block[0] // held_tenants
        term = lax.dynamic_index_in_dim(combined, owner_me, 0, keepdims=False)
        zero = jnp.zeros_like(term)
        own_sum = jnp.where(owner_me == me_dp, term, zero)
        cross_sum = jnp.where(owner_me == (me_dp ^ half), term, zero)
        for s in range(1, half):
            mate = me_dp ^ s
            outgoing = jnp.where((owner_me == mate) | (owner_me == (mate ^ half)), term, zero)
            arrived = lax.ppermute(outgoing, "dp", [(i, i ^ s) for i in range(dp_size)])
            sender_owner = tenants_seen[s] // held_tenants
            own_sum = own_sum + jnp.where(sender_owner == me_dp, arrived, zero)
            cross_sum = cross_sum + jnp.where(sender_owner == (me_dp ^ half), arrived, zero)
        arrived = lax.ppermute(cross_sum.astype(jnp.bfloat16), "dp", [(i, i ^ half) for i in range(dp_size)])
        grad_down = own_sum[:, :, :width_portion] + arrived[:, :, :width_portion].astype(jnp.float32)
        grad_up = own_sum[:, :, width_portion:] + arrived[:, :, width_portion:].astype(jnp.float32)
        return (grad_inputs, grad_down, grad_up)
    owned = lax.dynamic_index_in_dim(combined, me_dp, 0, keepdims=False)
    grad_down = owned[:, :, :width_portion]
    grad_up = owned[:, :, width_portion:]
    for shift, pairs in _partners(dp_size):
        outgoing = lax.dynamic_index_in_dim(combined, _dest_of(me_dp, shift, dp_size), 0, keepdims=False)
        arrived = lax.ppermute(outgoing.astype(jnp.bfloat16), "dp", pairs).astype(jnp.float32)
        grad_down = grad_down + arrived[:, :, :width_portion]
        grad_up = grad_up + arrived[:, :, width_portion:]
    return (grad_inputs, grad_down, grad_up)


def solution(mesh):
    in_specs = (
        P("dp", "tensor"),
        P("dp", "tensor"),
        P(None, "tensor"),
        P("dp", None, "tensor"),
        P("dp", None, "tensor"),
        P("dp"),
    )
    out_specs = (P("dp", "tensor"), P("dp", None, "tensor"), P("dp", None, "tensor"))
    return jax.shard_map(
        on_device, mesh=mesh, in_specs=in_specs, out_specs=out_specs, check_vma=False
    )
```

```python
import jax
import jax.numpy as jnp
from jax import lax
from jax.sharding import PartitionSpec as P

ADAPTER_SCALE = 2.0


def _partners(size):
    if size & (size - 1) == 0:
        return [(s, [(i, i ^ s) for i in range(size)]) for s in range(1, size)]
    return [(s, [(i, (i + s) % size) for i in range(size)]) for s in range(1, size)]


def _source_of(me, shift, size):
    if size & (size - 1) == 0:
        return me ^ shift
    return (me - shift + size) % size


def _dest_of(me, shift, size):
    if size & (size - 1) == 0:
        return me ^ shift
    return (me + shift) % size


def _gather_dp(local, axis, size):
    me = lax.axis_index(axis)
    if size & (size - 1) != 0 or size < 4:
        got = [local]
        sources = [me]
        for shift, pairs in _partners(size):
            got.append(lax.ppermute(local, axis, pairs))
            sources.append(_source_of(me, shift, size))
        return got, sources
    pair = jnp.concatenate([local, lax.ppermute(local, axis, [(i, i ^ 1) for i in range(size)])], 0)
    got = [pair]
    sources = [me, me ^ 1]
    for m in range(1, size // 2):
        shift = 2 * m
        got.append(lax.ppermute(pair, axis, [(i, i ^ shift) for i in range(size)]))
        sources += [me ^ shift, me ^ shift ^ 1]
    held = local.shape[0]
    pieces = []
    for g in got:
        pieces += [g[k * held:(k + 1) * held] for k in range(g.shape[0] // held)]
    return pieces, sources


def _psum_small(value, axis, size):
    if size & (size - 1) != 0:
        total = value
        for _, pairs in _partners(size):
            total = total + lax.ppermute(value, axis, pairs)
        return total
    total = value
    step = 1
    while step < size:
        total = total + lax.ppermute(total, axis, [(i, i ^ step) for i in range(size)])
        step *= 2
    return total


def _frozen_term(cotangent, weight, axis, size, ready=None):
    if size & (size - 1) != 0:
        partial = lax.dot_general(
            cotangent, weight, (((1,), (1,)), ((), ())), preferred_element_type=jnp.float32
        )
        return lax.psum_scatter(partial, axis, scatter_dimension=1, tiled=True), ready
    me = lax.axis_index(axis)
    rows = weight.shape[0] // size

    def term(block):
        piece = lax.dynamic_slice_in_dim(weight, block * rows, rows, axis=0)
        return lax.dot_general(
            cotangent, piece, (((1,), (1,)), ((), ())), preferred_element_type=jnp.float32
        )

    held = [term(me ^ e) for e in range(size)]
    step = 0
    while len(held) > 1:
        if step == 1 and ready is not None:
            *leaving, ready = lax.optimization_barrier((*held[1::2], ready))
            held[1::2] = leaving
        partner = 1 << step
        pairs = [(i, i ^ partner) for i in range(size)]
        got = [lax.ppermute(held[e], axis, pairs) for e in range(1, len(held), 2)]
        held = [held[e] + g for e, g in zip(range(0, len(held), 2), got)]
        step += 1
    return held[0], ready


def on_device(
    inputs, cotangent, frozen_key_weight, adapter_down_weight, adapter_up_weight, tenant_per_block
):
    token_row_count, width_portion = inputs.shape
    key_portion = cotangent.shape[1]
    block_count = tenant_per_block.shape[0]
    block_rows = token_row_count // block_count
    adapter_rank_size = adapter_down_weight.shape[1]
    held_tenants = adapter_down_weight.shape[0]
    dp_size = lax.axis_size("dp")
    tensor_size = lax.axis_size("tensor")
    tenant_number = dp_size * held_tenants
    me_dp = lax.axis_index("dp")


    packed = jnp.concatenate([adapter_down_weight, adapter_up_weight], axis=2)
    pieces, sources = _gather_dp(packed, "dp", dp_size)
    owner = tenant_per_block // held_tenants
    local = tenant_per_block % held_tenants
    selected = jnp.zeros((block_count,) + packed.shape[1:], packed.dtype)
    for piece, source in zip(pieces, sources):
        for k in range(held_tenants):
            hit = (owner == source) & (local == k)
            selected = jnp.where(hit[:, None, None], piece[k][None], selected)
    sel_down = selected[:, :, :width_portion]
    sel_up = selected[:, :, width_portion:]

    input_blocks = inputs.reshape(block_count, block_rows, width_portion)
    cotangent_blocks = cotangent.reshape(block_count, block_rows, key_portion)
    low_in = jnp.einsum("bnd,brd->bnr", input_blocks, sel_down, preferred_element_type=jnp.float32)
    reduced_output = ADAPTER_SCALE * jnp.einsum(
        "bnk,brk->bnr", cotangent_blocks, sel_up, preferred_element_type=jnp.float32
    )
    lows = jnp.concatenate([low_in, reduced_output], axis=2)
    base_grad, lows = _frozen_term(cotangent, frozen_key_weight, "tensor", tensor_size, lows)
    lows = _psum_small(lows, "tensor", tensor_size)
    reduced_input_batch = lows[:, :, :adapter_rank_size].astype(jnp.bfloat16)
    low_out_b = lows[:, :, adapter_rank_size:].astype(jnp.bfloat16)

    adapter_grad = jnp.einsum(
        "bnr,brd->bnd", low_out_b, sel_down, preferred_element_type=jnp.float32
    )
    adapter_grad = adapter_grad.reshape(token_row_count, width_portion)
    grad_inputs = (base_grad + adapter_grad).astype(jnp.bfloat16)

    all_tenants = jnp.arange(tenant_number, dtype=jnp.int32)
    member = tenant_per_block[:, None] == all_tenants[None, :]
    member_b = member.astype(jnp.bfloat16)
    weighted_out = (member_b[:, None, :, None] * low_out_b[:, :, None, :]).reshape(
        token_row_count, tenant_number * adapter_rank_size
    )
    weighted_in = (member_b[:, None, :, None] * reduced_input_batch[:, :, None, :]).reshape(
        token_row_count, tenant_number * adapter_rank_size
    )
    down_contribution = lax.dot_general(
        weighted_out, inputs, (((0,), (0,)), ((), ())), preferred_element_type=jnp.float32
    )
    up_contribution = ADAPTER_SCALE * lax.dot_general(
        weighted_in, cotangent, (((0,), (0,)), ((), ())), preferred_element_type=jnp.float32
    )
    down_contribution = down_contribution.reshape(dp_size, held_tenants, adapter_rank_size, width_portion)
    up_contribution = up_contribution.reshape(dp_size, held_tenants, adapter_rank_size, key_portion)
    combined = jnp.concatenate([down_contribution, up_contribution], axis=3)
    owned = lax.dynamic_index_in_dim(combined, me_dp, 0, keepdims=False)
    grad_down = owned[:, :, :width_portion]
    grad_up = owned[:, :, width_portion:]
    for shift, pairs in _partners(dp_size):
        outgoing = lax.dynamic_index_in_dim(combined, _dest_of(me_dp, shift, dp_size), 0, keepdims=False)
        arrived = lax.ppermute(outgoing.astype(jnp.bfloat16), "dp", pairs).astype(jnp.float32)
        grad_down = grad_down + arrived[:, :, :width_portion]
        grad_up = grad_up + arrived[:, :, width_portion:]
    return (grad_inputs, grad_down, grad_up)


def solution(mesh):
    in_specs = (
        P("dp", "tensor"),
        P("dp", "tensor"),
        P(None, "tensor"),
        P("dp", None, "tensor"),
        P("dp", None, "tensor"),
        P("dp"),
    )
    out_specs = (P("dp", "tensor"), P("dp", None, "tensor"), P("dp", None, "tensor"))
    return jax.shard_map(
        on_device, mesh=mesh, in_specs=in_specs, out_specs=out_specs, check_vma=False
    )
```

```python
import jax
import jax.numpy as jnp
from jax import lax
from jax.sharding import PartitionSpec as P

ADAPTER_SCALE = 2.0


def _partners(size):
    if size & (size - 1) == 0:
        return [(s, [(i, i ^ s) for i in range(size)]) for s in range(1, size)]
    return [(s, [(i, (i + s) % size) for i in range(size)]) for s in range(1, size)]


def _source_of(me, shift, size):
    if size & (size - 1) == 0:
        return me ^ shift
    return (me - shift + size) % size


def _dest_of(me, shift, size):
    if size & (size - 1) == 0:
        return me ^ shift
    return (me + shift) % size


def _gather_dp(local, axis, size):
    me = lax.axis_index(axis)
    if size & (size - 1) != 0 or size < 4:
        got = [local]
        sources = [me]
        for shift, pairs in _partners(size):
            got.append(lax.ppermute(local, axis, pairs))
            sources.append(_source_of(me, shift, size))
        return got, sources
    pair = jnp.concatenate([local, lax.ppermute(local, axis, [(i, i ^ 1) for i in range(size)])], 0)
    got = [pair]
    sources = [me, me ^ 1]
    for m in range(1, size // 2):
        shift = 2 * m
        got.append(lax.ppermute(pair, axis, [(i, i ^ shift) for i in range(size)]))
        sources += [me ^ shift, me ^ shift ^ 1]
    held = local.shape[0]
    pieces = []
    for g in got:
        pieces += [g[k * held:(k + 1) * held] for k in range(g.shape[0] // held)]
    return pieces, sources


def _psum_small(value, axis, size):
    if size & (size - 1) != 0:
        total = value
        for _, pairs in _partners(size):
            total = total + lax.ppermute(value, axis, pairs)
        return total
    total = value
    step = 1
    while step < size:
        total = total + lax.ppermute(total, axis, [(i, i ^ step) for i in range(size)])
        step *= 2
    return total


def _frozen_term(cotangent, weight, axis, size, ready=None):
    if size & (size - 1) != 0:
        partial = lax.dot_general(
            cotangent, weight, (((1,), (1,)), ((), ())), preferred_element_type=jnp.float32
        )
        return lax.psum_scatter(partial, axis, scatter_dimension=1, tiled=True), ready
    me = lax.axis_index(axis)
    rows = weight.shape[0] // size

    def term(block):
        piece = lax.dynamic_slice_in_dim(weight, block * rows, rows, axis=0)
        return lax.dot_general(
            cotangent, piece, (((1,), (1,)), ((), ())), preferred_element_type=jnp.float32
        )

    held = [term(me ^ e) for e in range(size)]
    step = 0
    while len(held) > 1:
        if step == 1 and ready is not None:
            *leaving, ready = lax.optimization_barrier((*held[1::2], ready))
            held[1::2] = leaving
        partner = 1 << step
        pairs = [(i, i ^ partner) for i in range(size)]
        got = [lax.ppermute(held[e], axis, pairs) for e in range(1, len(held), 2)]
        held = [held[e] + g for e, g in zip(range(0, len(held), 2), got)]
        step += 1
    return held[0], ready


def on_device(
    inputs, cotangent, frozen_key_weight, adapter_down_weight, adapter_up_weight, tenant_per_block
):
    token_row_count, width_portion = inputs.shape
    key_portion = cotangent.shape[1]
    block_count = tenant_per_block.shape[0]
    block_rows = token_row_count // block_count
    adapter_rank_size = adapter_down_weight.shape[1]
    held_tenants = adapter_down_weight.shape[0]
    dp_size = lax.axis_size("dp")
    tensor_size = lax.axis_size("tensor")
    tenant_number = dp_size * held_tenants
    me_dp = lax.axis_index("dp")


    packed = jnp.concatenate([adapter_down_weight, adapter_up_weight], axis=2)
    pieces, sources = _gather_dp(packed, "dp", dp_size)
    owner = tenant_per_block // held_tenants
    local = tenant_per_block % held_tenants
    selected = jnp.zeros((block_count,) + packed.shape[1:], packed.dtype)
    for piece, source in zip(pieces, sources):
        for k in range(held_tenants):
            hit = (owner == source) & (local == k)
            selected = jnp.where(hit[:, None, None], piece[k][None], selected)
    base_grad, selected = _frozen_term(cotangent, frozen_key_weight, "tensor", tensor_size, selected)
    sel_down = selected[:, :, :width_portion]
    sel_up = selected[:, :, width_portion:]

    input_blocks = inputs.reshape(block_count, block_rows, width_portion)
    cotangent_blocks = cotangent.reshape(block_count, block_rows, key_portion)
    low_in = jnp.einsum("bnd,brd->bnr", input_blocks, sel_down, preferred_element_type=jnp.float32)
    reduced_output = ADAPTER_SCALE * jnp.einsum(
        "bnk,brk->bnr", cotangent_blocks, sel_up, preferred_element_type=jnp.float32
    )
    lows = jnp.concatenate([low_in, reduced_output], axis=2)
    lows = _psum_small(lows, "tensor", tensor_size)
    reduced_input_batch = lows[:, :, :adapter_rank_size].astype(jnp.bfloat16)
    low_out_b = lows[:, :, adapter_rank_size:].astype(jnp.bfloat16)

    adapter_grad = jnp.einsum(
        "bnr,brd->bnd", low_out_b, sel_down, preferred_element_type=jnp.float32
    )
    adapter_grad = adapter_grad.reshape(token_row_count, width_portion)
    grad_inputs = (base_grad + adapter_grad).astype(jnp.bfloat16)

    all_tenants = jnp.arange(tenant_number, dtype=jnp.int32)
    member = tenant_per_block[:, None] == all_tenants[None, :]
    member_b = member.astype(jnp.bfloat16)
    weighted_out = (member_b[:, None, :, None] * low_out_b[:, :, None, :]).reshape(
        token_row_count, tenant_number * adapter_rank_size
    )
    weighted_in = (member_b[:, None, :, None] * reduced_input_batch[:, :, None, :]).reshape(
        token_row_count, tenant_number * adapter_rank_size
    )
    down_contribution = lax.dot_general(
        weighted_out, inputs, (((0,), (0,)), ((), ())), preferred_element_type=jnp.float32
    )
    up_contribution = ADAPTER_SCALE * lax.dot_general(
        weighted_in, cotangent, (((0,), (0,)), ((), ())), preferred_element_type=jnp.float32
    )
    down_contribution = down_contribution.reshape(dp_size, held_tenants, adapter_rank_size, width_portion)
    up_contribution = up_contribution.reshape(dp_size, held_tenants, adapter_rank_size, key_portion)
    combined = jnp.concatenate([down_contribution, up_contribution], axis=3)
    owned = lax.dynamic_index_in_dim(combined, me_dp, 0, keepdims=False)
    grad_down = owned[:, :, :width_portion]
    grad_up = owned[:, :, width_portion:]
    for shift, pairs in _partners(dp_size):
        outgoing = lax.dynamic_index_in_dim(combined, _dest_of(me_dp, shift, dp_size), 0, keepdims=False)
        arrived = lax.ppermute(outgoing.astype(jnp.bfloat16), "dp", pairs).astype(jnp.float32)
        grad_down = grad_down + arrived[:, :, :width_portion]
        grad_up = grad_up + arrived[:, :, width_portion:]
    return (grad_inputs, grad_down, grad_up)


def solution(mesh):
    in_specs = (
        P("dp", "tensor"),
        P("dp", "tensor"),
        P(None, "tensor"),
        P("dp", None, "tensor"),
        P("dp", None, "tensor"),
        P("dp"),
    )
    out_specs = (P("dp", "tensor"), P("dp", None, "tensor"), P("dp", None, "tensor"))
    return jax.shard_map(
        on_device, mesh=mesh, in_specs=in_specs, out_specs=out_specs, check_vma=False
    )
```

```python
import jax
import jax.numpy as jnp
from jax import lax
from jax.sharding import PartitionSpec as P

ADAPTER_SCALE = 2.0


def _partners(size):
    if size & (size - 1) == 0:
        return [(s, [(i, i ^ s) for i in range(size)]) for s in range(1, size)]
    return [(s, [(i, (i + s) % size) for i in range(size)]) for s in range(1, size)]


def _source_of(me, shift, size):
    if size & (size - 1) == 0:
        return me ^ shift
    return (me - shift + size) % size


def _dest_of(me, shift, size):
    if size & (size - 1) == 0:
        return me ^ shift
    return (me + shift) % size


def _gather_dp(local, axis, size):
    me = lax.axis_index(axis)
    if size & (size - 1) != 0 or size < 4:
        got = [local]
        sources = [me]
        for shift, pairs in _partners(size):
            got.append(lax.ppermute(local, axis, pairs))
            sources.append(_source_of(me, shift, size))
        return got, sources
    half = size // 2
    pair = jnp.concatenate([local, lax.ppermute(local, axis, [(i, i ^ half) for i in range(size)])], 0)
    got = [pair]
    sources = [me, me ^ half]
    for shift in range(1, half):
        got.append(lax.ppermute(pair, axis, [(i, i ^ shift) for i in range(size)]))
        sources += [me ^ shift, me ^ shift ^ half]
    held = local.shape[0]
    pieces = []
    for g in got:
        pieces += [g[k * held:(k + 1) * held] for k in range(g.shape[0] // held)]
    return pieces, sources


def _psum_small(value, axis, size):
    if size & (size - 1) != 0:
        total = value
        for _, pairs in _partners(size):
            total = total + lax.ppermute(value, axis, pairs)
        return total
    total = value
    step = 1
    while step < size:
        total = total + lax.ppermute(total, axis, [(i, i ^ step) for i in range(size)])
        step *= 2
    return total


def _frozen_term(cotangent, weight, axis, size, ready=None):
    if size & (size - 1) != 0:
        partial = lax.dot_general(
            cotangent, weight, (((1,), (1,)), ((), ())), preferred_element_type=jnp.float32
        )
        return lax.psum_scatter(partial, axis, scatter_dimension=1, tiled=True), ready
    me = lax.axis_index(axis)
    rows = weight.shape[0] // size

    def term(block):
        piece = lax.dynamic_slice_in_dim(weight, block * rows, rows, axis=0)
        return lax.dot_general(
            cotangent, piece, (((1,), (1,)), ((), ())), preferred_element_type=jnp.float32
        )

    held = [term(me ^ e) for e in range(size)]
    step = 0
    while len(held) > 1:
        if step == 1 and ready is not None:
            *leaving, ready = lax.optimization_barrier((*held[1::2], ready))
            held[1::2] = leaving
        partner = 1 << step
        pairs = [(i, i ^ partner) for i in range(size)]
        got = [lax.ppermute(held[e], axis, pairs) for e in range(1, len(held), 2)]
        held = [held[e] + g for e, g in zip(range(0, len(held), 2), got)]
        step += 1
    return held[0], ready


def on_device(
    inputs, cotangent, frozen_key_weight, adapter_down_weight, adapter_up_weight, tenant_per_block
):
    token_row_count, width_portion = inputs.shape
    key_portion = cotangent.shape[1]
    block_count = tenant_per_block.shape[0]
    block_rows = token_row_count // block_count
    adapter_rank_size = adapter_down_weight.shape[1]
    held_tenants = adapter_down_weight.shape[0]
    dp_size = lax.axis_size("dp")
    tensor_size = lax.axis_size("tensor")
    tenant_number = dp_size * held_tenants
    me_dp = lax.axis_index("dp")


    packed = jnp.concatenate([adapter_down_weight, adapter_up_weight], axis=2)
    pieces, sources = _gather_dp(packed, "dp", dp_size)
    owner = tenant_per_block // held_tenants
    local = tenant_per_block % held_tenants
    selected = jnp.zeros((block_count,) + packed.shape[1:], packed.dtype)
    for piece, source in zip(pieces, sources):
        for k in range(held_tenants):
            hit = (owner == source) & (local == k)
            selected = jnp.where(hit[:, None, None], piece[k][None], selected)
    sel_down = selected[:, :, :width_portion]
    sel_up = selected[:, :, width_portion:]

    input_blocks = inputs.reshape(block_count, block_rows, width_portion)
    cotangent_blocks = cotangent.reshape(block_count, block_rows, key_portion)
    low_in = jnp.einsum("bnd,brd->bnr", input_blocks, sel_down, preferred_element_type=jnp.float32)
    reduced_output = ADAPTER_SCALE * jnp.einsum(
        "bnk,brk->bnr", cotangent_blocks, sel_up, preferred_element_type=jnp.float32
    )
    lows = jnp.concatenate([low_in, reduced_output], axis=2)
    base_grad, lows = _frozen_term(cotangent, frozen_key_weight, "tensor", tensor_size, lows)
    lows = _psum_small(lows, "tensor", tensor_size)
    reduced_input_batch = lows[:, :, :adapter_rank_size].astype(jnp.bfloat16)
    low_out_b = lows[:, :, adapter_rank_size:].astype(jnp.bfloat16)

    adapter_grad = jnp.einsum(
        "bnr,brd->bnd", low_out_b, sel_down, preferred_element_type=jnp.float32
    )
    adapter_grad = adapter_grad.reshape(token_row_count, width_portion)
    grad_inputs = (base_grad + adapter_grad).astype(jnp.bfloat16)

    all_tenants = jnp.arange(tenant_number, dtype=jnp.int32)
    member = tenant_per_block[:, None] == all_tenants[None, :]
    member_b = member.astype(jnp.bfloat16)
    weighted_out = (member_b[:, None, :, None] * low_out_b[:, :, None, :]).reshape(
        token_row_count, tenant_number * adapter_rank_size
    )
    weighted_in = (member_b[:, None, :, None] * reduced_input_batch[:, :, None, :]).reshape(
        token_row_count, tenant_number * adapter_rank_size
    )
    down_contribution = lax.dot_general(
        weighted_out, inputs, (((0,), (0,)), ((), ())), preferred_element_type=jnp.float32
    )
    up_contribution = ADAPTER_SCALE * lax.dot_general(
        weighted_in, cotangent, (((0,), (0,)), ((), ())), preferred_element_type=jnp.float32
    )
    down_contribution = down_contribution.reshape(dp_size, held_tenants, adapter_rank_size, width_portion)
    up_contribution = up_contribution.reshape(dp_size, held_tenants, adapter_rank_size, key_portion)
    combined = jnp.concatenate([down_contribution, up_contribution], axis=3)
    owned = lax.dynamic_index_in_dim(combined, me_dp, 0, keepdims=False)
    grad_down = owned[:, :, :width_portion]
    grad_up = owned[:, :, width_portion:]
    for shift, pairs in _partners(dp_size):
        outgoing = lax.dynamic_index_in_dim(combined, _dest_of(me_dp, shift, dp_size), 0, keepdims=False)
        arrived = lax.ppermute(outgoing.astype(jnp.bfloat16), "dp", pairs).astype(jnp.float32)
        grad_down = grad_down + arrived[:, :, :width_portion]
        grad_up = grad_up + arrived[:, :, width_portion:]
    return (grad_inputs, grad_down, grad_up)


def solution(mesh):
    in_specs = (
        P("dp", "tensor"),
        P("dp", "tensor"),
        P(None, "tensor"),
        P("dp", None, "tensor"),
        P("dp", None, "tensor"),
        P("dp"),
    )
    out_specs = (P("dp", "tensor"), P("dp", None, "tensor"), P("dp", None, "tensor"))
    return jax.shard_map(
        on_device, mesh=mesh, in_specs=in_specs, out_specs=out_specs, check_vma=False
    )
```

```python
import jax
import jax.numpy as jnp
from jax import lax
from jax.sharding import PartitionSpec as P

ADAPTER_SCALE = 2.0


def _partners(size):
    if size & (size - 1) == 0:
        return [(s, [(i, i ^ s) for i in range(size)]) for s in range(1, size)]
    return [(s, [(i, (i + s) % size) for i in range(size)]) for s in range(1, size)]


def _source_of(me, shift, size):
    if size & (size - 1) == 0:
        return me ^ shift
    return (me - shift + size) % size


def _dest_of(me, shift, size):
    if size & (size - 1) == 0:
        return me ^ shift
    return (me + shift) % size


def _gather_dp(local, axis, size):
    me = lax.axis_index(axis)
    if size & (size - 1) != 0 or size < 4:
        got = [local]
        sources = [me]
        for shift, pairs in _partners(size):
            got.append(lax.ppermute(local, axis, pairs))
            sources.append(_source_of(me, shift, size))
        return got, sources
    half = size // 2
    pair = jnp.concatenate([local, lax.ppermute(local, axis, [(i, i ^ half) for i in range(size)])], 0)
    got = [pair]
    sources = [me, me ^ half]
    for shift in range(1, half):
        got.append(lax.ppermute(pair, axis, [(i, i ^ shift) for i in range(size)]))
        sources += [me ^ shift, me ^ shift ^ half]
    held = local.shape[0]
    pieces = []
    for g in got:
        pieces += [g[k * held:(k + 1) * held] for k in range(g.shape[0] // held)]
    return pieces, sources


def _psum_small(value, axis, size):
    if size & (size - 1) != 0:
        total = value
        for _, pairs in _partners(size):
            total = total + lax.ppermute(value, axis, pairs)
        return total
    total = value
    step = 1
    while step < size:
        total = total + lax.ppermute(total, axis, [(i, i ^ step) for i in range(size)])
        step *= 2
    return total


def _frozen_term(cotangent, weight, axis, size, ready=None):
    if size & (size - 1) != 0:
        partial = lax.dot_general(
            cotangent, weight, (((1,), (1,)), ((), ())), preferred_element_type=jnp.float32
        )
        return lax.psum_scatter(partial, axis, scatter_dimension=1, tiled=True), ready
    me = lax.axis_index(axis)
    rows = weight.shape[0] // size

    def term(block):
        piece = lax.dynamic_slice_in_dim(weight, block * rows, rows, axis=0)
        return lax.dot_general(
            cotangent, piece, (((1,), (1,)), ((), ())), preferred_element_type=jnp.float32
        )

    held = [term(me ^ e) for e in range(size)]
    step = 0
    while len(held) > 1:
        if step == 1 and ready is not None:
            *leaving, ready = lax.optimization_barrier((*held[1::2], ready))
            held[1::2] = leaving
        partner = 1 << step
        pairs = [(i, i ^ partner) for i in range(size)]
        got = [lax.ppermute(held[e], axis, pairs) for e in range(1, len(held), 2)]
        held = [held[e] + g for e, g in zip(range(0, len(held), 2), got)]
        step += 1
    return held[0], ready


def on_device(
    inputs, cotangent, frozen_key_weight, adapter_down_weight, adapter_up_weight, tenant_per_block
):
    token_row_count, width_portion = inputs.shape
    key_portion = cotangent.shape[1]
    block_count = tenant_per_block.shape[0]
    block_rows = token_row_count // block_count
    adapter_rank_size = adapter_down_weight.shape[1]
    held_tenants = adapter_down_weight.shape[0]
    dp_size = lax.axis_size("dp")
    tensor_size = lax.axis_size("tensor")
    tenant_number = dp_size * held_tenants
    me_dp = lax.axis_index("dp")


    packed = jnp.concatenate([adapter_down_weight, adapter_up_weight], axis=2)
    width = packed.shape[2]
    routed = block_count == 1 and dp_size >= 4 and dp_size & (dp_size - 1) == 0
    if routed:
        tenant = tenant_per_block[0]
        digits = jnp.zeros((held_tenants, adapter_rank_size, 128), jnp.float32)
        digits = digits.at[:, 0, 0].set((tenant // 256).astype(jnp.float32))
        digits = digits.at[:, 0, 1].set((tenant % 256).astype(jnp.float32))
        packed = jnp.concatenate([packed, digits.astype(packed.dtype)], axis=2)
    pieces, sources = _gather_dp(packed, "dp", dp_size)
    if routed:
        mates_tenant = [
            pieces[2 * m][0, 0, width].astype(jnp.int32) * 256 + pieces[2 * m][0, 0, width + 1].astype(jnp.int32)
            for m in range(dp_size // 2)
        ]
        pieces = [q[..., :width] for q in pieces]
        packed = packed[..., :width]
    owner = tenant_per_block // held_tenants
    local = tenant_per_block % held_tenants
    selected = jnp.zeros((block_count,) + packed.shape[1:], packed.dtype)
    for piece, source in zip(pieces, sources):
        for k in range(held_tenants):
            hit = (owner == source) & (local == k)
            selected = jnp.where(hit[:, None, None], piece[k][None], selected)
    sel_down = selected[:, :, :width_portion]
    sel_up = selected[:, :, width_portion:]

    input_blocks = inputs.reshape(block_count, block_rows, width_portion)
    cotangent_blocks = cotangent.reshape(block_count, block_rows, key_portion)
    low_in = jnp.einsum("bnd,brd->bnr", input_blocks, sel_down, preferred_element_type=jnp.float32)
    reduced_output = ADAPTER_SCALE * jnp.einsum(
        "bnk,brk->bnr", cotangent_blocks, sel_up, preferred_element_type=jnp.float32
    )
    lows = jnp.concatenate([low_in, reduced_output], axis=2)
    base_grad, lows = _frozen_term(cotangent, frozen_key_weight, "tensor", tensor_size, lows)
    lows = _psum_small(lows, "tensor", tensor_size)
    reduced_input_batch = lows[:, :, :adapter_rank_size].astype(jnp.bfloat16)
    low_out_b = lows[:, :, adapter_rank_size:].astype(jnp.bfloat16)

    adapter_grad = jnp.einsum(
        "bnr,brd->bnd", low_out_b, sel_down, preferred_element_type=jnp.float32
    )
    adapter_grad = adapter_grad.reshape(token_row_count, width_portion)
    grad_inputs = (base_grad + adapter_grad).astype(jnp.bfloat16)

    all_tenants = jnp.arange(tenant_number, dtype=jnp.int32)
    member = tenant_per_block[:, None] == all_tenants[None, :]
    member_b = member.astype(jnp.bfloat16)
    weighted_out = (member_b[:, None, :, None] * low_out_b[:, :, None, :]).reshape(
        token_row_count, tenant_number * adapter_rank_size
    )
    weighted_in = (member_b[:, None, :, None] * reduced_input_batch[:, :, None, :]).reshape(
        token_row_count, tenant_number * adapter_rank_size
    )
    down_contribution = lax.dot_general(
        weighted_out, inputs, (((0,), (0,)), ((), ())), preferred_element_type=jnp.float32
    )
    up_contribution = ADAPTER_SCALE * lax.dot_general(
        weighted_in, cotangent, (((0,), (0,)), ((), ())), preferred_element_type=jnp.float32
    )
    down_contribution = down_contribution.reshape(dp_size, held_tenants, adapter_rank_size, width_portion)
    up_contribution = up_contribution.reshape(dp_size, held_tenants, adapter_rank_size, key_portion)
    combined = jnp.concatenate([down_contribution, up_contribution], axis=3)
    if routed:
        half = dp_size // 2
        owner_me = tenant_per_block[0] // held_tenants
        term = lax.dynamic_index_in_dim(combined, owner_me, 0, keepdims=False)
        zero = jnp.zeros_like(term)
        own_sum = jnp.where(owner_me == me_dp, term, zero)
        cross_sum = jnp.where(owner_me == (me_dp ^ half), term, zero)
        for m in range(1, half):
            mate = me_dp ^ m
            outgoing = jnp.where((owner_me == mate) | (owner_me == (mate ^ half)), term, zero)
            arrived = lax.ppermute(outgoing, "dp", [(i, i ^ m) for i in range(dp_size)])
            sender_owner = mates_tenant[m] // held_tenants
            own_sum = own_sum + jnp.where(sender_owner == me_dp, arrived, zero)
            cross_sum = cross_sum + jnp.where(sender_owner == (me_dp ^ half), arrived, zero)
        arrived = lax.ppermute(cross_sum.astype(jnp.bfloat16), "dp", [(i, i ^ half) for i in range(dp_size)])
        grad_down = own_sum[:, :, :width_portion] + arrived[:, :, :width_portion].astype(jnp.float32)
        grad_up = own_sum[:, :, width_portion:] + arrived[:, :, width_portion:].astype(jnp.float32)
        return (grad_inputs, grad_down, grad_up)
    owned = lax.dynamic_index_in_dim(combined, me_dp, 0, keepdims=False)
    grad_down = owned[:, :, :width_portion]
    grad_up = owned[:, :, width_portion:]
    for shift, pairs in _partners(dp_size):
        outgoing = lax.dynamic_index_in_dim(combined, _dest_of(me_dp, shift, dp_size), 0, keepdims=False)
        arrived = lax.ppermute(outgoing.astype(jnp.bfloat16), "dp", pairs).astype(jnp.float32)
        grad_down = grad_down + arrived[:, :, :width_portion]
        grad_up = grad_up + arrived[:, :, width_portion:]
    return (grad_inputs, grad_down, grad_up)


def solution(mesh):
    in_specs = (
        P("dp", "tensor"),
        P("dp", "tensor"),
        P(None, "tensor"),
        P("dp", None, "tensor"),
        P("dp", None, "tensor"),
        P("dp"),
    )
    out_specs = (P("dp", "tensor"), P("dp", None, "tensor"), P("dp", None, "tensor"))
    return jax.shard_map(
        on_device, mesh=mesh, in_specs=in_specs, out_specs=out_specs, check_vma=False
    )
```

```python
import jax
import jax.numpy as jnp
from jax import lax
from jax.sharding import PartitionSpec as P

ADAPTER_SCALE = 2.0


def _partners(size):
    if size & (size - 1) == 0:
        return [(s, [(i, i ^ s) for i in range(size)]) for s in range(1, size)]
    return [(s, [(i, (i + s) % size) for i in range(size)]) for s in range(1, size)]


def _source_of(me, shift, size):
    if size & (size - 1) == 0:
        return me ^ shift
    return (me - shift + size) % size


def _dest_of(me, shift, size):
    if size & (size - 1) == 0:
        return me ^ shift
    return (me + shift) % size


def _gather_dp(local, axis, size):
    me = lax.axis_index(axis)
    if size & (size - 1) != 0 or size < 4:
        got = [local]
        sources = [me]
        for shift, pairs in _partners(size):
            got.append(lax.ppermute(local, axis, pairs))
            sources.append(_source_of(me, shift, size))
        return got, sources
    half = size // 2
    pair = jnp.concatenate([local, lax.ppermute(local, axis, [(i, i ^ half) for i in range(size)])], 0)
    got = [pair]
    sources = [me, me ^ half]
    for shift in range(1, half):
        got.append(lax.ppermute(pair, axis, [(i, i ^ shift) for i in range(size)]))
        sources += [me ^ shift, me ^ shift ^ half]
    held = local.shape[0]
    pieces = []
    for g in got:
        pieces += [g[k * held:(k + 1) * held] for k in range(g.shape[0] // held)]
    return pieces, sources


def _psum_small(value, axis, size):
    if size & (size - 1) != 0:
        total = value
        for _, pairs in _partners(size):
            total = total + lax.ppermute(value, axis, pairs)
        return total
    total = value
    step = 1
    while step < size:
        total = total + lax.ppermute(total, axis, [(i, i ^ step) for i in range(size)])
        step *= 2
    return total


def _frozen_term(cotangent, weight, axis, size, ready=None):
    if size & (size - 1) != 0:
        partial = lax.dot_general(
            cotangent, weight, (((1,), (1,)), ((), ())), preferred_element_type=jnp.float32
        )
        return (lax.psum_scatter(partial, axis, scatter_dimension=1, tiled=True), None), ready
    me = lax.axis_index(axis)
    rows = weight.shape[0] // size

    def term(block):
        piece = lax.dynamic_slice_in_dim(weight, block * rows, rows, axis=0)
        return lax.dot_general(
            cotangent, piece, (((1,), (1,)), ((), ())), preferred_element_type=jnp.float32
        )

    held = [term(me ^ e) for e in range(size)]
    step = 0
    while len(held) > 1:
        if step == 1 and ready is not None:
            *leaving, ready = lax.optimization_barrier((*held[1::2], ready))
            held[1::2] = leaving
        partner = 1 << step
        pairs = [(i, i ^ partner) for i in range(size)]
        got = [lax.ppermute(held[e], axis, pairs) for e in range(1, len(held), 2)]
        if len(held) == 2:
            return (held[0], got[0]), ready
        held = [held[e] + g for e, g in zip(range(0, len(held), 2), got)]
        step += 1
    return (held[0], None), ready


def on_device(
    inputs, cotangent, frozen_key_weight, adapter_down_weight, adapter_up_weight, tenant_per_block
):
    token_row_count, width_portion = inputs.shape
    key_portion = cotangent.shape[1]
    block_count = tenant_per_block.shape[0]
    block_rows = token_row_count // block_count
    adapter_rank_size = adapter_down_weight.shape[1]
    held_tenants = adapter_down_weight.shape[0]
    dp_size = lax.axis_size("dp")
    tensor_size = lax.axis_size("tensor")
    tenant_number = dp_size * held_tenants
    me_dp = lax.axis_index("dp")


    packed = jnp.concatenate([adapter_down_weight, adapter_up_weight], axis=2)
    pieces, sources = _gather_dp(packed, "dp", dp_size)
    owner = tenant_per_block // held_tenants
    local = tenant_per_block % held_tenants
    selected = jnp.zeros((block_count,) + packed.shape[1:], packed.dtype)
    for piece, source in zip(pieces, sources):
        for k in range(held_tenants):
            hit = (owner == source) & (local == k)
            selected = jnp.where(hit[:, None, None], piece[k][None], selected)
    sel_down = selected[:, :, :width_portion]
    sel_up = selected[:, :, width_portion:]

    input_blocks = inputs.reshape(block_count, block_rows, width_portion)
    cotangent_blocks = cotangent.reshape(block_count, block_rows, key_portion)
    low_in = jnp.einsum("bnd,brd->bnr", input_blocks, sel_down, preferred_element_type=jnp.float32)
    reduced_output = ADAPTER_SCALE * jnp.einsum(
        "bnk,brk->bnr", cotangent_blocks, sel_up, preferred_element_type=jnp.float32
    )
    lows = jnp.concatenate([low_in, reduced_output], axis=2)
    (own_grad, far_grad), lows = _frozen_term(cotangent, frozen_key_weight, "tensor", tensor_size, lows)
    lows = _psum_small(lows, "tensor", tensor_size)
    reduced_input_batch = lows[:, :, :adapter_rank_size].astype(jnp.bfloat16)
    low_out_b = lows[:, :, adapter_rank_size:].astype(jnp.bfloat16)
    if far_grad is None:
        base_grad = own_grad
    else:
        own_grad, low_out_b = lax.optimization_barrier((own_grad, low_out_b))
        base_grad = own_grad + far_grad

    adapter_grad = jnp.einsum(
        "bnr,brd->bnd", low_out_b, sel_down, preferred_element_type=jnp.float32
    )
    adapter_grad = adapter_grad.reshape(token_row_count, width_portion)
    grad_inputs = (base_grad + adapter_grad).astype(jnp.bfloat16)

    all_tenants = jnp.arange(tenant_number, dtype=jnp.int32)
    member = tenant_per_block[:, None] == all_tenants[None, :]
    member_b = member.astype(jnp.bfloat16)
    weighted_out = (member_b[:, None, :, None] * low_out_b[:, :, None, :]).reshape(
        token_row_count, tenant_number * adapter_rank_size
    )
    weighted_in = (member_b[:, None, :, None] * reduced_input_batch[:, :, None, :]).reshape(
        token_row_count, tenant_number * adapter_rank_size
    )
    down_contribution = lax.dot_general(
        weighted_out, inputs, (((0,), (0,)), ((), ())), preferred_element_type=jnp.float32
    )
    up_contribution = ADAPTER_SCALE * lax.dot_general(
        weighted_in, cotangent, (((0,), (0,)), ((), ())), preferred_element_type=jnp.float32
    )
    down_contribution = down_contribution.reshape(dp_size, held_tenants, adapter_rank_size, width_portion)
    up_contribution = up_contribution.reshape(dp_size, held_tenants, adapter_rank_size, key_portion)
    combined = jnp.concatenate([down_contribution, up_contribution], axis=3)
    owned = lax.dynamic_index_in_dim(combined, me_dp, 0, keepdims=False)
    grad_down = owned[:, :, :width_portion]
    grad_up = owned[:, :, width_portion:]
    for shift, pairs in _partners(dp_size):
        outgoing = lax.dynamic_index_in_dim(combined, _dest_of(me_dp, shift, dp_size), 0, keepdims=False)
        arrived = lax.ppermute(outgoing.astype(jnp.bfloat16), "dp", pairs).astype(jnp.float32)
        grad_down = grad_down + arrived[:, :, :width_portion]
        grad_up = grad_up + arrived[:, :, width_portion:]
    return (grad_inputs, grad_down, grad_up)


def solution(mesh):
    in_specs = (
        P("dp", "tensor"),
        P("dp", "tensor"),
        P(None, "tensor"),
        P("dp", None, "tensor"),
        P("dp", None, "tensor"),
        P("dp"),
    )
    out_specs = (P("dp", "tensor"), P("dp", None, "tensor"), P("dp", None, "tensor"))
    return jax.shard_map(
        on_device, mesh=mesh, in_specs=in_specs, out_specs=out_specs, check_vma=False
    )
```

```python
import jax
import jax.numpy as jnp
from jax import lax
from jax.sharding import PartitionSpec as P

ADAPTER_SCALE = 2.0


def _partners(size):
    if size & (size - 1) == 0:
        return [(s, [(i, i ^ s) for i in range(size)]) for s in range(1, size)]
    return [(s, [(i, (i + s) % size) for i in range(size)]) for s in range(1, size)]


def _source_of(me, shift, size):
    if size & (size - 1) == 0:
        return me ^ shift
    return (me - shift + size) % size


def _dest_of(me, shift, size):
    if size & (size - 1) == 0:
        return me ^ shift
    return (me + shift) % size


def _gather_dp(local, axis, size):
    me = lax.axis_index(axis)
    if size & (size - 1) != 0 or size < 4:
        got = [local]
        sources = [me]
        for shift, pairs in _partners(size):
            got.append(lax.ppermute(local, axis, pairs))
            sources.append(_source_of(me, shift, size))
        return got, sources
    held_now = local
    sources = [me]
    shift = size // 2
    while shift >= 1:
        held_now = jnp.concatenate(
            [held_now, lax.ppermute(held_now, axis, [(i, i ^ shift) for i in range(size)])], 0
        )
        sources = sources + [src ^ shift for src in sources]
        shift //= 2
    got = [held_now]
    held = local.shape[0]
    pieces = []
    for g in got:
        pieces += [g[k * held:(k + 1) * held] for k in range(g.shape[0] // held)]
    return pieces, sources


def _psum_small(value, axis, size):
    if size & (size - 1) != 0:
        total = value
        for _, pairs in _partners(size):
            total = total + lax.ppermute(value, axis, pairs)
        return total
    total = value
    step = 1
    while step < size:
        total = total + lax.ppermute(total, axis, [(i, i ^ step) for i in range(size)])
        step *= 2
    return total


def _frozen_term(cotangent, weight, axis, size, ready=None):
    if size & (size - 1) != 0:
        partial = lax.dot_general(
            cotangent, weight, (((1,), (1,)), ((), ())), preferred_element_type=jnp.float32
        )
        return lax.psum_scatter(partial, axis, scatter_dimension=1, tiled=True), ready
    me = lax.axis_index(axis)
    rows = weight.shape[0] // size

    def term(block):
        piece = lax.dynamic_slice_in_dim(weight, block * rows, rows, axis=0)
        return lax.dot_general(
            cotangent, piece, (((1,), (1,)), ((), ())), preferred_element_type=jnp.float32
        )

    held = [term(me ^ e) for e in range(size)]
    step = 0
    while len(held) > 1:
        if step == 1 and ready is not None:
            *leaving, ready = lax.optimization_barrier((*held[1::2], ready))
            held[1::2] = leaving
        partner = 1 << step
        pairs = [(i, i ^ partner) for i in range(size)]
        got = [lax.ppermute(held[e], axis, pairs) for e in range(1, len(held), 2)]
        held = [held[e] + g for e, g in zip(range(0, len(held), 2), got)]
        step += 1
    return held[0], ready


def on_device(
    inputs, cotangent, frozen_key_weight, adapter_down_weight, adapter_up_weight, tenant_per_block
):
    token_row_count, width_portion = inputs.shape
    key_portion = cotangent.shape[1]
    block_count = tenant_per_block.shape[0]
    block_rows = token_row_count // block_count
    adapter_rank_size = adapter_down_weight.shape[1]
    held_tenants = adapter_down_weight.shape[0]
    dp_size = lax.axis_size("dp")
    tensor_size = lax.axis_size("tensor")
    tenant_number = dp_size * held_tenants
    me_dp = lax.axis_index("dp")


    packed = jnp.concatenate([adapter_down_weight, adapter_up_weight], axis=2)
    pieces, sources = _gather_dp(packed, "dp", dp_size)
    owner = tenant_per_block // held_tenants
    local = tenant_per_block % held_tenants
    selected = jnp.zeros((block_count,) + packed.shape[1:], packed.dtype)
    for piece, source in zip(pieces, sources):
        for k in range(held_tenants):
            hit = (owner == source) & (local == k)
            selected = jnp.where(hit[:, None, None], piece[k][None], selected)
    sel_down = selected[:, :, :width_portion]
    sel_up = selected[:, :, width_portion:]

    input_blocks = inputs.reshape(block_count, block_rows, width_portion)
    cotangent_blocks = cotangent.reshape(block_count, block_rows, key_portion)
    low_in = jnp.einsum("bnd,brd->bnr", input_blocks, sel_down, preferred_element_type=jnp.float32)
    reduced_output = ADAPTER_SCALE * jnp.einsum(
        "bnk,brk->bnr", cotangent_blocks, sel_up, preferred_element_type=jnp.float32
    )
    lows = jnp.concatenate([low_in, reduced_output], axis=2)
    base_grad, lows = _frozen_term(cotangent, frozen_key_weight, "tensor", tensor_size, lows)
    lows = _psum_small(lows, "tensor", tensor_size)
    reduced_input_batch = lows[:, :, :adapter_rank_size].astype(jnp.bfloat16)
    low_out_b = lows[:, :, adapter_rank_size:].astype(jnp.bfloat16)

    adapter_grad = jnp.einsum(
        "bnr,brd->bnd", low_out_b, sel_down, preferred_element_type=jnp.float32
    )
    adapter_grad = adapter_grad.reshape(token_row_count, width_portion)
    grad_inputs = (base_grad + adapter_grad).astype(jnp.bfloat16)

    all_tenants = jnp.arange(tenant_number, dtype=jnp.int32)
    member = tenant_per_block[:, None] == all_tenants[None, :]
    member_b = member.astype(jnp.bfloat16)
    weighted_out = (member_b[:, None, :, None] * low_out_b[:, :, None, :]).reshape(
        token_row_count, tenant_number * adapter_rank_size
    )
    weighted_in = (member_b[:, None, :, None] * reduced_input_batch[:, :, None, :]).reshape(
        token_row_count, tenant_number * adapter_rank_size
    )
    down_contribution = lax.dot_general(
        weighted_out, inputs, (((0,), (0,)), ((), ())), preferred_element_type=jnp.float32
    )
    up_contribution = ADAPTER_SCALE * lax.dot_general(
        weighted_in, cotangent, (((0,), (0,)), ((), ())), preferred_element_type=jnp.float32
    )
    down_contribution = down_contribution.reshape(dp_size, held_tenants, adapter_rank_size, width_portion)
    up_contribution = up_contribution.reshape(dp_size, held_tenants, adapter_rank_size, key_portion)
    combined = jnp.concatenate([down_contribution, up_contribution], axis=3)
    owned = lax.dynamic_index_in_dim(combined, me_dp, 0, keepdims=False)
    grad_down = owned[:, :, :width_portion]
    grad_up = owned[:, :, width_portion:]
    for shift, pairs in _partners(dp_size):
        outgoing = lax.dynamic_index_in_dim(combined, _dest_of(me_dp, shift, dp_size), 0, keepdims=False)
        arrived = lax.ppermute(outgoing.astype(jnp.bfloat16), "dp", pairs).astype(jnp.float32)
        grad_down = grad_down + arrived[:, :, :width_portion]
        grad_up = grad_up + arrived[:, :, width_portion:]
    return (grad_inputs, grad_down, grad_up)


def solution(mesh):
    in_specs = (
        P("dp", "tensor"),
        P("dp", "tensor"),
        P(None, "tensor"),
        P("dp", None, "tensor"),
        P("dp", None, "tensor"),
        P("dp"),
    )
    out_specs = (P("dp", "tensor"), P("dp", None, "tensor"), P("dp", None, "tensor"))
    return jax.shard_map(
        on_device, mesh=mesh, in_specs=in_specs, out_specs=out_specs, check_vma=False
    )
```

```python
import jax
import jax.numpy as jnp
from jax import lax
from jax.sharding import PartitionSpec as P

ADAPTER_SCALE = 2.0


def _partners(size):
    if size & (size - 1) == 0:
        return [(s, [(i, i ^ s) for i in range(size)]) for s in range(1, size)]
    return [(s, [(i, (i + s) % size) for i in range(size)]) for s in range(1, size)]


def _source_of(me, shift, size):
    if size & (size - 1) == 0:
        return me ^ shift
    return (me - shift + size) % size


def _dest_of(me, shift, size):
    if size & (size - 1) == 0:
        return me ^ shift
    return (me + shift) % size


def _gather_dp(local, axis, size):
    me = lax.axis_index(axis)
    if size & (size - 1) != 0 or size < 4:
        got = [local]
        sources = [me]
        for shift, pairs in _partners(size):
            got.append(lax.ppermute(local, axis, pairs))
            sources.append(_source_of(me, shift, size))
        return got, sources
    half = size // 2
    pair = jnp.concatenate([local, lax.ppermute(local, axis, [(i, i ^ half) for i in range(size)])], 0)
    got = [pair]
    sources = [me, me ^ half]
    for shift in range(1, half):
        got.append(lax.ppermute(pair, axis, [(i, i ^ shift) for i in range(size)]))
        sources += [me ^ shift, me ^ shift ^ half]
    held = local.shape[0]
    pieces = []
    for g in got:
        pieces += [g[k * held:(k + 1) * held] for k in range(g.shape[0] // held)]
    return pieces, sources


def _psum_small(value, axis, size):
    if size & (size - 1) != 0:
        total = value
        for _, pairs in _partners(size):
            total = total + lax.ppermute(value, axis, pairs)
        return total
    total = value
    step = 1
    while step < size:
        total = total + lax.ppermute(total, axis, [(i, i ^ step) for i in range(size)])
        step *= 2
    return total


def _frozen_term(cotangent, weight, axis, size, ready=None):
    if size & (size - 1) != 0 or size == 1:
        partial = lax.dot_general(
            cotangent, weight, (((1,), (1,)), ((), ())), preferred_element_type=jnp.float32
        )
        return lax.psum_scatter(partial, axis, scatter_dimension=1, tiled=True), ready
    me = lax.axis_index(axis)
    rows = weight.shape[0] // size

    def term(block):
        piece = lax.dynamic_slice_in_dim(weight, block * rows, rows, axis=0)
        return lax.dot_general(
            cotangent, piece, (((1,), (1,)), ((), ())), preferred_element_type=jnp.float32
        )

    pieces = [lax.dynamic_slice_in_dim(weight, (me ^ e) * rows, rows, axis=0) for e in range(1, size, 2)]
    leaving = jnp.einsum(
        "nk,bdk->bnd", cotangent, jnp.stack(pieces, 0), preferred_element_type=jnp.float32
    )
    got = lax.ppermute(leaving, axis, [(i, i ^ 1) for i in range(size)])
    held = [term(me ^ e) + got[m] for m, e in enumerate(range(0, size, 2))]
    step = 1
    while len(held) > 1:
        if step == 1 and ready is not None:
            *leaving, ready = lax.optimization_barrier((*held[1::2], ready))
            held[1::2] = leaving
        partner = 1 << step
        pairs = [(i, i ^ partner) for i in range(size)]
        got = [lax.ppermute(held[e], axis, pairs) for e in range(1, len(held), 2)]
        held = [held[e] + g for e, g in zip(range(0, len(held), 2), got)]
        step += 1
    return held[0], ready


def on_device(
    inputs, cotangent, frozen_key_weight, adapter_down_weight, adapter_up_weight, tenant_per_block
):
    token_row_count, width_portion = inputs.shape
    key_portion = cotangent.shape[1]
    block_count = tenant_per_block.shape[0]
    block_rows = token_row_count // block_count
    adapter_rank_size = adapter_down_weight.shape[1]
    held_tenants = adapter_down_weight.shape[0]
    dp_size = lax.axis_size("dp")
    tensor_size = lax.axis_size("tensor")
    tenant_number = dp_size * held_tenants
    me_dp = lax.axis_index("dp")


    packed = jnp.concatenate([adapter_down_weight, adapter_up_weight], axis=2)
    pieces, sources = _gather_dp(packed, "dp", dp_size)
    owner = tenant_per_block // held_tenants
    local = tenant_per_block % held_tenants
    selected = jnp.zeros((block_count,) + packed.shape[1:], packed.dtype)
    for piece, source in zip(pieces, sources):
        for k in range(held_tenants):
            hit = (owner == source) & (local == k)
            selected = jnp.where(hit[:, None, None], piece[k][None], selected)
    sel_down = selected[:, :, :width_portion]
    sel_up = selected[:, :, width_portion:]

    input_blocks = inputs.reshape(block_count, block_rows, width_portion)
    cotangent_blocks = cotangent.reshape(block_count, block_rows, key_portion)
    low_in = jnp.einsum("bnd,brd->bnr", input_blocks, sel_down, preferred_element_type=jnp.float32)
    reduced_output = ADAPTER_SCALE * jnp.einsum(
        "bnk,brk->bnr", cotangent_blocks, sel_up, preferred_element_type=jnp.float32
    )
    lows = jnp.concatenate([low_in, reduced_output], axis=2)
    base_grad, lows = _frozen_term(cotangent, frozen_key_weight, "tensor", tensor_size, lows)
    lows = _psum_small(lows, "tensor", tensor_size)
    reduced_input_batch = lows[:, :, :adapter_rank_size].astype(jnp.bfloat16)
    low_out_b = lows[:, :, adapter_rank_size:].astype(jnp.bfloat16)

    adapter_grad = jnp.einsum(
        "bnr,brd->bnd", low_out_b, sel_down, preferred_element_type=jnp.float32
    )
    adapter_grad = adapter_grad.reshape(token_row_count, width_portion)
    grad_inputs = (base_grad + adapter_grad).astype(jnp.bfloat16)

    all_tenants = jnp.arange(tenant_number, dtype=jnp.int32)
    member = tenant_per_block[:, None] == all_tenants[None, :]
    member_b = member.astype(jnp.bfloat16)
    weighted_out = (member_b[:, None, :, None] * low_out_b[:, :, None, :]).reshape(
        token_row_count, tenant_number * adapter_rank_size
    )
    weighted_in = (member_b[:, None, :, None] * reduced_input_batch[:, :, None, :]).reshape(
        token_row_count, tenant_number * adapter_rank_size
    )
    down_contribution = lax.dot_general(
        weighted_out, inputs, (((0,), (0,)), ((), ())), preferred_element_type=jnp.float32
    )
    up_contribution = ADAPTER_SCALE * lax.dot_general(
        weighted_in, cotangent, (((0,), (0,)), ((), ())), preferred_element_type=jnp.float32
    )
    down_contribution = down_contribution.reshape(dp_size, held_tenants, adapter_rank_size, width_portion)
    up_contribution = up_contribution.reshape(dp_size, held_tenants, adapter_rank_size, key_portion)
    combined = jnp.concatenate([down_contribution, up_contribution], axis=3)
    owned = lax.dynamic_index_in_dim(combined, me_dp, 0, keepdims=False)
    grad_down = owned[:, :, :width_portion]
    grad_up = owned[:, :, width_portion:]
    for shift, pairs in _partners(dp_size):
        outgoing = lax.dynamic_index_in_dim(combined, _dest_of(me_dp, shift, dp_size), 0, keepdims=False)
        arrived = lax.ppermute(outgoing.astype(jnp.bfloat16), "dp", pairs).astype(jnp.float32)
        grad_down = grad_down + arrived[:, :, :width_portion]
        grad_up = grad_up + arrived[:, :, width_portion:]
    return (grad_inputs, grad_down, grad_up)


def solution(mesh):
    in_specs = (
        P("dp", "tensor"),
        P("dp", "tensor"),
        P(None, "tensor"),
        P("dp", None, "tensor"),
        P("dp", None, "tensor"),
        P("dp"),
    )
    out_specs = (P("dp", "tensor"), P("dp", None, "tensor"), P("dp", None, "tensor"))
    return jax.shard_map(
        on_device, mesh=mesh, in_specs=in_specs, out_specs=out_specs, check_vma=False
    )
```

```python
import jax
import jax.numpy as jnp
from jax import lax
from jax.sharding import PartitionSpec as P

ADAPTER_SCALE = 2.0


def _partners(size):
    if size & (size - 1) == 0:
        return [(s, [(i, i ^ s) for i in range(size)]) for s in range(1, size)]
    return [(s, [(i, (i + s) % size) for i in range(size)]) for s in range(1, size)]


def _source_of(me, shift, size):
    if size & (size - 1) == 0:
        return me ^ shift
    return (me - shift + size) % size


def _dest_of(me, shift, size):
    if size & (size - 1) == 0:
        return me ^ shift
    return (me + shift) % size


def _gather_dp(local, axis, size):
    me = lax.axis_index(axis)
    if size & (size - 1) != 0 or size < 4:
        got = [local]
        sources = [me]
        for shift, pairs in _partners(size):
            got.append(lax.ppermute(local, axis, pairs))
            sources.append(_source_of(me, shift, size))
        return got, sources
    half = size // 2
    pair = jnp.concatenate([local, lax.ppermute(local, axis, [(i, i ^ half) for i in range(size)])], 0)
    got = [pair]
    sources = [me, me ^ half]
    for shift in range(1, half):
        got.append(lax.ppermute(pair, axis, [(i, i ^ shift) for i in range(size)]))
        sources += [me ^ shift, me ^ shift ^ half]
    held = local.shape[0]
    pieces = []
    for g in got:
        pieces += [g[k * held:(k + 1) * held] for k in range(g.shape[0] // held)]
    return pieces, sources


def _psum_small(value, axis, size):
    if True:
        total = value
        for _, pairs in _partners(size):
            total = total + lax.ppermute(value, axis, pairs)
        return total
    total = value
    step = 1
    while step < size:
        total = total + lax.ppermute(total, axis, [(i, i ^ step) for i in range(size)])
        step *= 2
    return total


def _frozen_term(cotangent, weight, axis, size, ready=None):
    if size & (size - 1) != 0:
        partial = lax.dot_general(
            cotangent, weight, (((1,), (1,)), ((), ())), preferred_element_type=jnp.float32
        )
        return lax.psum_scatter(partial, axis, scatter_dimension=1, tiled=True), ready
    me = lax.axis_index(axis)
    rows = weight.shape[0] // size

    def term(block):
        piece = lax.dynamic_slice_in_dim(weight, block * rows, rows, axis=0)
        return lax.dot_general(
            cotangent, piece, (((1,), (1,)), ((), ())), preferred_element_type=jnp.float32
        )

    held = [term(me ^ e) for e in range(size)]
    step = 0
    while len(held) > 1:
        if step == 1 and ready is not None:
            *leaving, ready = lax.optimization_barrier((*held[1::2], ready))
            held[1::2] = leaving
        partner = 1 << step
        pairs = [(i, i ^ partner) for i in range(size)]
        got = [lax.ppermute(held[e], axis, pairs) for e in range(1, len(held), 2)]
        held = [held[e] + g for e, g in zip(range(0, len(held), 2), got)]
        step += 1
    return held[0], ready


def on_device(
    inputs, cotangent, frozen_key_weight, adapter_down_weight, adapter_up_weight, tenant_per_block
):
    token_row_count, width_portion = inputs.shape
    key_portion = cotangent.shape[1]
    block_count = tenant_per_block.shape[0]
    block_rows = token_row_count // block_count
    adapter_rank_size = adapter_down_weight.shape[1]
    held_tenants = adapter_down_weight.shape[0]
    dp_size = lax.axis_size("dp")
    tensor_size = lax.axis_size("tensor")
    tenant_number = dp_size * held_tenants
    me_dp = lax.axis_index("dp")


    packed = jnp.concatenate([adapter_down_weight, adapter_up_weight], axis=2)
    pieces, sources = _gather_dp(packed, "dp", dp_size)
    owner = tenant_per_block // held_tenants
    local = tenant_per_block % held_tenants
    selected = jnp.zeros((block_count,) + packed.shape[1:], packed.dtype)
    for piece, source in zip(pieces, sources):
        for k in range(held_tenants):
            hit = (owner == source) & (local == k)
            selected = jnp.where(hit[:, None, None], piece[k][None], selected)
    sel_down = selected[:, :, :width_portion]
    sel_up = selected[:, :, width_portion:]

    input_blocks = inputs.reshape(block_count, block_rows, width_portion)
    cotangent_blocks = cotangent.reshape(block_count, block_rows, key_portion)
    low_in = jnp.einsum("bnd,brd->bnr", input_blocks, sel_down, preferred_element_type=jnp.float32)
    reduced_output = ADAPTER_SCALE * jnp.einsum(
        "bnk,brk->bnr", cotangent_blocks, sel_up, preferred_element_type=jnp.float32
    )
    lows = jnp.concatenate([low_in, reduced_output], axis=2)
    base_grad, lows = _frozen_term(cotangent, frozen_key_weight, "tensor", tensor_size, lows)
    lows = _psum_small(lows, "tensor", tensor_size)
    reduced_input_batch = lows[:, :, :adapter_rank_size].astype(jnp.bfloat16)
    low_out_b = lows[:, :, adapter_rank_size:].astype(jnp.bfloat16)

    adapter_grad = jnp.einsum(
        "bnr,brd->bnd", low_out_b, sel_down, preferred_element_type=jnp.float32
    )
    adapter_grad = adapter_grad.reshape(token_row_count, width_portion)
    grad_inputs = (base_grad + adapter_grad).astype(jnp.bfloat16)

    all_tenants = jnp.arange(tenant_number, dtype=jnp.int32)
    member = tenant_per_block[:, None] == all_tenants[None, :]
    member_b = member.astype(jnp.bfloat16)
    weighted_out = (member_b[:, None, :, None] * low_out_b[:, :, None, :]).reshape(
        token_row_count, tenant_number * adapter_rank_size
    )
    weighted_in = (member_b[:, None, :, None] * reduced_input_batch[:, :, None, :]).reshape(
        token_row_count, tenant_number * adapter_rank_size
    )
    down_contribution = lax.dot_general(
        weighted_out, inputs, (((0,), (0,)), ((), ())), preferred_element_type=jnp.float32
    )
    up_contribution = ADAPTER_SCALE * lax.dot_general(
        weighted_in, cotangent, (((0,), (0,)), ((), ())), preferred_element_type=jnp.float32
    )
    down_contribution = down_contribution.reshape(dp_size, held_tenants, adapter_rank_size, width_portion)
    up_contribution = up_contribution.reshape(dp_size, held_tenants, adapter_rank_size, key_portion)
    combined = jnp.concatenate([down_contribution, up_contribution], axis=3)
    owned = lax.dynamic_index_in_dim(combined, me_dp, 0, keepdims=False)
    grad_down = owned[:, :, :width_portion]
    grad_up = owned[:, :, width_portion:]
    for shift, pairs in _partners(dp_size):
        outgoing = lax.dynamic_index_in_dim(combined, _dest_of(me_dp, shift, dp_size), 0, keepdims=False)
        arrived = lax.ppermute(outgoing.astype(jnp.bfloat16), "dp", pairs).astype(jnp.float32)
        grad_down = grad_down + arrived[:, :, :width_portion]
        grad_up = grad_up + arrived[:, :, width_portion:]
    return (grad_inputs, grad_down, grad_up)


def solution(mesh):
    in_specs = (
        P("dp", "tensor"),
        P("dp", "tensor"),
        P(None, "tensor"),
        P("dp", None, "tensor"),
        P("dp", None, "tensor"),
        P("dp"),
    )
    out_specs = (P("dp", "tensor"), P("dp", None, "tensor"), P("dp", None, "tensor"))
    return jax.shard_map(
        on_device, mesh=mesh, in_specs=in_specs, out_specs=out_specs, check_vma=False
    )
```

```python
import jax
import jax.numpy as jnp
from jax import lax
from jax.sharding import PartitionSpec as P

ADAPTER_SCALE = 2.0


def _partners(size):
    if size & (size - 1) == 0:
        return [(s, [(i, i ^ s) for i in range(size)]) for s in range(1, size)]
    return [(s, [(i, (i + s) % size) for i in range(size)]) for s in range(1, size)]


def _source_of(me, shift, size):
    if size & (size - 1) == 0:
        return me ^ shift
    return (me - shift + size) % size


def _dest_of(me, shift, size):
    if size & (size - 1) == 0:
        return me ^ shift
    return (me + shift) % size


def _gather_dp(local, axis, size):
    me = lax.axis_index(axis)
    if size & (size - 1) != 0 or size < 4:
        got = [local]
        sources = [me]
        for shift, pairs in _partners(size):
            got.append(lax.ppermute(local, axis, pairs))
            sources.append(_source_of(me, shift, size))
        return got, sources
    half = size // 2
    pair = jnp.concatenate([local, lax.ppermute(local, axis, [(i, i ^ half) for i in range(size)])], 0)
    got = [pair]
    sources = [me, me ^ half]
    for shift in range(1, half):
        got.append(lax.ppermute(pair, axis, [(i, i ^ shift) for i in range(size)]))
        sources += [me ^ shift, me ^ shift ^ half]
    held = local.shape[0]
    pieces = []
    for g in got:
        pieces += [g[k * held:(k + 1) * held] for k in range(g.shape[0] // held)]
    return pieces, sources


def _psum_small(value, axis, size):
    if True:
        total = value
        for _, pairs in _partners(size):
            total = total + lax.ppermute(value, axis, pairs)
        return total
    total = value
    step = 1
    while step < size:
        total = total + lax.ppermute(total, axis, [(i, i ^ step) for i in range(size)])
        step *= 2
    return total


def _frozen_term(cotangent, weight, axis, size, ready=None):
    if size & (size - 1) != 0:
        partial = lax.dot_general(
            cotangent, weight, (((1,), (1,)), ((), ())), preferred_element_type=jnp.float32
        )
        return lax.psum_scatter(partial, axis, scatter_dimension=1, tiled=True), ready
    me = lax.axis_index(axis)
    rows = weight.shape[0] // size

    def term(block):
        piece = lax.dynamic_slice_in_dim(weight, block * rows, rows, axis=0)
        return lax.dot_general(
            cotangent, piece, (((1,), (1,)), ((), ())), preferred_element_type=jnp.float32
        )

    held = [term(me ^ e) for e in range(size)]
    step = 0
    while len(held) > 1:
        if step == 1 and ready is not None:
            *leaving, ready = lax.optimization_barrier((*held[1::2], ready))
            held[1::2] = leaving
        partner = 1 << step
        pairs = [(i, i ^ partner) for i in range(size)]
        got = [lax.ppermute(held[e], axis, pairs) for e in range(1, len(held), 2)]
        held = [held[e] + g for e, g in zip(range(0, len(held), 2), got)]
        step += 1
    return held[0], ready


def on_device(
    inputs, cotangent, frozen_key_weight, adapter_down_weight, adapter_up_weight, tenant_per_block
):
    token_row_count, width_portion = inputs.shape
    key_portion = cotangent.shape[1]
    block_count = tenant_per_block.shape[0]
    block_rows = token_row_count // block_count
    adapter_rank_size = adapter_down_weight.shape[1]
    held_tenants = adapter_down_weight.shape[0]
    dp_size = lax.axis_size("dp")
    tensor_size = lax.axis_size("tensor")
    tenant_number = dp_size * held_tenants
    me_dp = lax.axis_index("dp")


    packed = jnp.concatenate([adapter_down_weight, adapter_up_weight], axis=2)
    pieces, sources = _gather_dp(packed, "dp", dp_size)
    owner = tenant_per_block // held_tenants
    local = tenant_per_block % held_tenants
    selected = jnp.zeros((block_count,) + packed.shape[1:], packed.dtype)
    for piece, source in zip(pieces, sources):
        for k in range(held_tenants):
            hit = (owner == source) & (local == k)
            selected = jnp.where(hit[:, None, None], piece[k][None], selected)
    sel_down = selected[:, :, :width_portion]
    sel_up = selected[:, :, width_portion:]

    input_blocks = inputs.reshape(block_count, block_rows, width_portion)
    cotangent_blocks = cotangent.reshape(block_count, block_rows, key_portion)
    low_in = jnp.einsum("bnd,brd->bnr", input_blocks, sel_down, preferred_element_type=jnp.float32)
    reduced_output = ADAPTER_SCALE * jnp.einsum(
        "bnk,brk->bnr", cotangent_blocks, sel_up, preferred_element_type=jnp.float32
    )
    lows = jnp.concatenate([low_in, reduced_output], axis=2)
    base_grad, lows = _frozen_term(cotangent, frozen_key_weight, "tensor", tensor_size, lows)
    lows = _psum_small(lows, "tensor", tensor_size)
    reduced_input_batch = lows[:, :, :adapter_rank_size].astype(jnp.bfloat16)
    low_out_b = lows[:, :, adapter_rank_size:].astype(jnp.bfloat16)

    adapter_grad = jnp.einsum(
        "bnr,brd->bnd", low_out_b, sel_down, preferred_element_type=jnp.float32
    )
    adapter_grad = adapter_grad.reshape(token_row_count, width_portion)
    grad_inputs = (base_grad + adapter_grad).astype(jnp.bfloat16)

    all_tenants = jnp.arange(tenant_number, dtype=jnp.int32)
    member = tenant_per_block[:, None] == all_tenants[None, :]
    member_b = member.astype(jnp.bfloat16)
    weighted_out = (member_b[:, None, :, None] * low_out_b[:, :, None, :]).reshape(
        token_row_count, tenant_number * adapter_rank_size
    )
    weighted_in = (member_b[:, None, :, None] * reduced_input_batch[:, :, None, :]).reshape(
        token_row_count, tenant_number * adapter_rank_size
    )
    down_contribution = lax.dot_general(
        weighted_out, inputs, (((0,), (0,)), ((), ())), preferred_element_type=jnp.float32
    )
    up_contribution = ADAPTER_SCALE * lax.dot_general(
        weighted_in, cotangent, (((0,), (0,)), ((), ())), preferred_element_type=jnp.float32
    )
    down_contribution = down_contribution.reshape(dp_size, held_tenants, adapter_rank_size, width_portion)
    up_contribution = up_contribution.reshape(dp_size, held_tenants, adapter_rank_size, key_portion)
    combined = jnp.concatenate([down_contribution, up_contribution], axis=3)
    owned = lax.dynamic_index_in_dim(combined, me_dp, 0, keepdims=False)
    grad_down = owned[:, :, :width_portion]
    grad_up = owned[:, :, width_portion:]
    for shift, pairs in sorted(_partners(dp_size), key=lambda sp: -sp[0]):
        outgoing = lax.dynamic_index_in_dim(combined, _dest_of(me_dp, shift, dp_size), 0, keepdims=False)
        arrived = lax.ppermute(outgoing.astype(jnp.bfloat16), "dp", pairs).astype(jnp.float32)
        grad_down = grad_down + arrived[:, :, :width_portion]
        grad_up = grad_up + arrived[:, :, width_portion:]
    return (grad_inputs, grad_down, grad_up)


def solution(mesh):
    in_specs = (
        P("dp", "tensor"),
        P("dp", "tensor"),
        P(None, "tensor"),
        P("dp", None, "tensor"),
        P("dp", None, "tensor"),
        P("dp"),
    )
    out_specs = (P("dp", "tensor"), P("dp", None, "tensor"), P("dp", None, "tensor"))
    return jax.shard_map(
        on_device, mesh=mesh, in_specs=in_specs, out_specs=out_specs, check_vma=False
    )
```
